32 devices in a mesh: slab: 8 (over z, y), chan: 4 (over x, core).
Axes of the slice: x: 2, y: 2, z: 4, core: 2. Of those that a mesh axis runs over, the one named last changes fastest.
Arguments:
- image: bfloat16 [32, 256, 1024], P('slab', None, 'chan'), may hold values from -6 to 6
- weight: bfloat16 [3, 3, 1024, 1024], P(None, None, None, 'chan'), may hold values from -0.0625 to 0.0625
- grad_out: bfloat16 [32, 256, 1024], P('slab', 'chan'), may hold values from -6 to 6
Outputs:
- normed: bfloat16 [32, 256, 1024], P('slab', 'chan')
- grad_input: bfloat16 [32, 256, 1024], P('slab', None, 'chan')
- grad_weight: float32 [3, 3, 1024, 1024], P(None, None, 'slab', 'chan')
The draws below stay inside these ranges and needn't reach their ends.
All inputs are finite; a program needn't handle non-finite values.
Results may differ from the reference program's by a relative error of at most 0.012.
Values may be sent and summed in bfloat16 or wider, within the bound.
No kernel may reach another device: no remote copies, remote signals or barrier semaphores. Data moves between devices by JAX's collectives and lax.ppermute only.
A program may use at most 128 MiB of HBM per device.

```python
import jax
import jax.numpy as jnp
from jax import lax

C = 1024
F = 1024
COLS = 256
HEIGHT = 32


def strengthened(entries, stream_key, source, target, blocks, factor):
    def block_of(dim):
        return (jnp.arange(entries.shape[dim]) // (entries.shape[dim] // blocks)).reshape((-1,) + (1,) * (entries.ndim - 1 - dim))

    first = jax.random.permutation(stream_key, blocks)[block_of(target)]
    other_side = (block_of(target) + blocks // 2) % blocks
    return jnp.where((block_of(source) == first) | (block_of(source) == other_side), factor * entries, entries)


def block_levels(stream_key, shape, shards, least, top_value):
    factor_of = 1.0
    for dim, parts in shards:
        steps = jax.random.uniform(jax.random.fold_in(jax.random.fold_in(stream_key, 6), dim), (parts,), jnp.float32, least / len(shards), top_value / len(shards))
        factor_of = factor_of * jnp.repeat(jnp.exp(steps), shape[dim] // parts).reshape((-1,) + (1,) * (len(shape) - 1 - dim))
    return factor_of


def gaussian(stream_key, shape, scale, bound, shards=(), kind=jnp.bfloat16):
    loudness = block_levels(stream_key, shape, shards, -0.22, 0.18) if shards else 1.0
    result = jax.random.normal(stream_key, shape, jnp.float32) * scale * loudness
    return jnp.minimum(jnp.maximum(result, -bound), bound).astype(kind)


def bell_draw_with(own_key, shape, scale, reach, shards, heavy, kind=jnp.bfloat16):
    values = scale * jax.random.normal(own_key, shape, jnp.float32)
    if shards:
        values = values * block_levels(own_key, shape, shards, -0.22, 0.18)
    return jnp.clip(strengthened(values, jax.random.fold_in(own_key, 3), *heavy), -reach, reach).astype(kind)


def setup_inputs(seed: int = 0) -> dict:
    keys = jax.random.split(jax.random.key(seed), 4)
    image = bell_draw_with(keys[0], (HEIGHT, COLS, C), 1.0, 6.0, ((0, 8), (2, 4)), (0, 2, 8, 2.0))
    weight = gaussian(keys[1], (3, 3, C, F), (9 * C) ** -0.5, 0.0625, ((3, 4),))
    grad_out = gaussian(keys[2], (HEIGHT, COLS, F), 1.0, 6.0, ((0, 8), (1, 4)))
    return dict(image=image, weight=weight, grad_out=grad_out)


def reference(image, weight, grad_out):
    weight_wide = weight.astype(jnp.float32)
    padded = jnp.pad(image.astype(jnp.float32), ((1, 1), (1, 1), (0, 0)))
    height = image.shape[0]
    breadth = image.shape[1]
    conv_sum = jnp.zeros((height, breadth, weight.shape[3]), jnp.float32)
    for tap_row in range(3):
        for tap_col in range(3):
            window = padded[tap_row:tap_row + height, tap_col:tap_col + breadth]
            conv_sum = conv_sum + jnp.einsum('hwc,cf->hwf', window, weight_wide[tap_row, tap_col])
    conv_out = conv_sum.astype(jnp.bfloat16).astype(jnp.float32)
    inverse_rms = lax.rsqrt(lax.optimization_barrier(jnp.mean(conv_out * conv_out, axis=-1, keepdims=True)) + 1e-06)
    unit = conv_out * inverse_rms
    normed = unit.astype(jnp.bfloat16)
    upstream = grad_out.astype(jnp.float32)
    grad_conv = (inverse_rms * (upstream - unit * lax.optimization_barrier(jnp.mean(upstream * unit, axis=-1, keepdims=True)))).astype(jnp.bfloat16)
    grad_wide = grad_conv.astype(jnp.float32)
    grad_padded = jnp.pad(grad_wide, ((1, 1), (1, 1), (0, 0)))
    input_sum = jnp.zeros((height, breadth, weight.shape[2]), jnp.float32)
    weight_rows = []
    for tap_row in range(3):
        for tap_col in range(3):
            window = grad_padded[2 - tap_row:2 - tap_row + height, 2 - tap_col:2 - tap_col + breadth]
            input_sum = input_sum + jnp.einsum('hwf,cf->hwc', window, weight_wide[tap_row, tap_col])
            source = padded[tap_row:tap_row + height, tap_col:tap_col + breadth]
            weight_rows.append(jnp.einsum('hwc,hwf->cf', source, grad_wide))
    grad_weight = jnp.stack(weight_rows).reshape(3, 3, weight.shape[2], weight.shape[3])
    return (normed, input_sum.astype(jnp.bfloat16), grad_weight)
```

```python
import jax
import jax.numpy as jnp
from jax import lax
from jax.sharding import PartitionSpec as P


def with_halo(cells, sides, width):
    for axis, dim in sides:
        count = lax.axis_size(axis)
        ends = count - 1
        head = lax.slice_in_dim(cells, 0, width, axis=dim)
        tail = lax.slice_in_dim(cells, cells.shape[dim] - width, cells.shape[dim], axis=dim)
        cells = jnp.concatenate(
            [
                lax.ppermute(tail, axis, [(i, (i + 1) % count) for i in range(ends)]),
                cells,
                lax.ppermute(head, axis, [((i + 1) % count, i) for i in range(ends)]),
            ],
            axis=dim,
        )
    return cells


def on_device(image, weight, grad_out):
    height = image.shape[0]
    breadth = image.shape[1]
    all_chans = weight.shape[2]
    local_filters = weight.shape[3]
    all_filters = local_filters * lax.axis_size("chan")
    slabs = lax.axis_size("slab")

    grad_filters = lax.all_to_all(grad_out, "chan", split_axis=2, concat_axis=1, tiled=True)

    rimmed = with_halo(image, (("slab", 0),), 1)
    padded = jnp.pad(rimmed, ((0, 0), (1, 1), (0, 0)))
    shard_piece = lax.all_gather(padded, "chan", axis=2, tiled=True)
    width_in = shard_piece.shape[2]

    core_rows = shard_piece[1 : 1 + height]
    column_image = lax.all_to_all(core_rows, "slab", split_axis=2, concat_axis=0, tiled=True)
    column_image = jnp.pad(column_image, ((1, 1), (0, 0), (0, 0)))

    running = jnp.zeros((height * breadth, local_filters), jnp.float32)
    for forward_tap_row in range(3):
        for forward_tap_col in range(3):
            forward_window = shard_piece[
                forward_tap_row : forward_tap_row + height,
                forward_tap_col : forward_tap_col + breadth,
            ].reshape(height * breadth, width_in)
            taps = weight[forward_tap_row, forward_tap_col]
            running = running + jnp.dot(forward_window, taps, preferred_element_type=jnp.float32)
    conv_out = running.astype(jnp.bfloat16).reshape(height, breadth, local_filters)

    conv_wide = conv_out.astype(jnp.float32)
    upstream = grad_filters.astype(jnp.float32)
    partial = jnp.stack(
        [jnp.sum(conv_wide * conv_wide, axis=-1), jnp.sum(upstream * conv_wide, axis=-1)], axis=-1
    )
    totals = lax.psum(partial, "chan")
    inverse_rms = lax.rsqrt(totals[..., 0:1] / all_filters + 1e-06)
    mean_gu = inverse_rms * (totals[..., 1:2] / all_filters)
    unit = conv_wide * inverse_rms
    normed_filters = unit.astype(jnp.bfloat16)
    grad_conv = (inverse_rms * (upstream - unit * mean_gu)).astype(jnp.bfloat16)
    normed = lax.all_to_all(normed_filters, "chan", split_axis=1, concat_axis=2, tiled=True)

    grad_rows = lax.all_gather(grad_conv, "slab", axis=0, tiled=True)
    total_rows = grad_rows.shape[0]
    grad_rows_flat = grad_rows.reshape(total_rows * breadth, local_filters)
    width_w = column_image.shape[2]
    blocks = []
    for weight_tap_row in range(3):
        for weight_tap_col in range(3):
            weight_window = column_image[
                weight_tap_row : weight_tap_row + total_rows,
                weight_tap_col : weight_tap_col + breadth,
            ].reshape(total_rows * breadth, width_w)
            blocks.append(
                lax.dot_general(
                    weight_window,
                    grad_rows_flat,
                    (((0,), (0,)), ((), ())),
                    preferred_element_type=jnp.float32,
                )
            )
    grad_weight = jnp.stack(blocks).reshape(3, 3, width_w, local_filters)

    grad_rimmed = with_halo(grad_conv, (("slab", 0),), 1)
    grad_padded = jnp.pad(grad_rimmed, ((0, 0), (1, 1), (0, 0)))
    input_term = jnp.zeros((height * breadth, all_chans), jnp.float32)
    for tap_row in range(3):
        for tap_col in range(3):
            window = grad_padded[
                2 - tap_row : 2 - tap_row + height, 2 - tap_col : 2 - tap_col + breadth
            ].reshape(height * breadth, local_filters)
            input_term = input_term + lax.dot_general(
                window,
                weight[tap_row, tap_col],
                (((1,), (1,)), ((), ())),
                preferred_element_type=jnp.float32,
            )
    grad_input = lax.psum_scatter(
        input_term.reshape(height, breadth, all_chans).astype(jnp.bfloat16),
        "chan",
        scatter_dimension=2,
        tiled=True,
    )
    return (normed, grad_input, grad_weight)


def solution(mesh):
    return jax.shard_map(
        on_device,
        mesh=mesh,
        in_specs=(P("slab", None, "chan"), P(None, None, None, "chan"), P("slab", "chan", None)),
        out_specs=(P("slab", "chan", None), P("slab", None, "chan"), P(None, None, "slab", "chan")),
        check_vma=False,
    )
```

```python
import jax
import jax.numpy as jnp
from jax import lax
from jax.sharding import Mesh
from jax.sharding import PartitionSpec as P

SLAB = ("hi", "lo")


def shift_rows(rows, upward):
    count = lax.axis_size(SLAB)
    if upward:
        pairs = [((i + 1), i) for i in range(count - 1)]
    else:
        pairs = [(i, i + 1) for i in range(count - 1)]
    return lax.ppermute(rows, SLAB, pairs)


def with_halo(cells):
    top = shift_rows(cells[-1:], upward=False)
    bottom = shift_rows(cells[:1], upward=True)
    return jnp.concatenate([top, cells, bottom], axis=0)


def conv(lhs, rhs, rhs_spec):
    out = lax.conv_general_dilated(
        lhs[None],
        rhs,
        window_strides=(1, 1),
        padding=((0, 0), (1, 1)),
        dimension_numbers=("NHWC", rhs_spec, "NHWC"),
        preferred_element_type=jnp.float32,
    )
    return out[0]


def on_device(image, weight, grad_out):
    height = image.shape[0]
    breadth = image.shape[1]
    all_chans = weight.shape[2]
    local_filters = weight.shape[3]
    chans = lax.axis_size("chan")
    all_filters = local_filters * chans
    n_hi = lax.axis_size("hi")
    n_lo = lax.axis_size("lo")
    lo = lax.axis_index("lo")
    piece = all_chans // (n_hi * n_lo)

    grad_filters = lax.all_to_all(grad_out, "chan", split_axis=2, concat_axis=1, tiled=True)

    gathered = lax.all_gather(image, "chan", axis=2, tiled=True)
    edges = jnp.concatenate(
        [shift_rows(image[-1:], upward=False), shift_rows(image[:1], upward=True)], axis=0
    )
    edges = lax.all_gather(edges, "chan", axis=2, tiled=True)
    rows6 = jnp.concatenate([edges[0:1], gathered, edges[1:2]], axis=0)

    def subset(x, which):
        shaped = x.reshape(x.shape[0], x.shape[1], n_hi, n_lo, piece)
        taken = lax.dynamic_index_in_dim(shaped, which, axis=3, keepdims=False)
        return taken.reshape(x.shape[0], x.shape[1], n_hi * piece)

    send_rows = lax.dynamic_slice_in_dim(rows6, 2 * lo, height, axis=0)
    sent_img = lax.ppermute(subset(send_rows, 1 - lo), "lo", [(0, 1), (1, 0)])

    conv_out = conv(rows6, weight, "HWIO").astype(jnp.bfloat16)

    conv_wide = conv_out.astype(jnp.float32)
    upstream = grad_filters.astype(jnp.float32)
    partial = jnp.stack(
        [jnp.sum(conv_wide * conv_wide, axis=-1), jnp.sum(upstream * conv_wide, axis=-1)], axis=-1
    )
    totals = lax.psum(partial, "chan")
    inverse_rms = lax.rsqrt(totals[..., 0:1] / all_filters + 1e-06)
    mean_gu = inverse_rms * (totals[..., 1:2] / all_filters)
    unit = conv_wide * inverse_rms
    normed_filters = unit.astype(jnp.bfloat16)
    grad_conv = (inverse_rms * (upstream - unit * mean_gu)).astype(jnp.bfloat16)
    normed = lax.all_to_all(normed_filters, "chan", split_axis=1, concat_axis=2, tiled=True)

    sent_grad = lax.ppermute(grad_conv, "lo", [(0, 1), (1, 0)])
    own_img = subset(rows6, lo)
    img_block = lax.dynamic_slice_in_dim(
        jnp.concatenate([sent_img, own_img, sent_img], axis=0), height * (1 - lo), 2 * height + 2, axis=0
    )
    img_block = jnp.pad(img_block, ((0, 0), (1, 1), (0, 0)))
    grad_block = lax.dynamic_slice_in_dim(
        jnp.concatenate([sent_grad, grad_conv, sent_grad], axis=0), height * (1 - lo), 2 * height, axis=0
    )
    pair_rows = 2 * height
    grad_flat = grad_block.reshape(pair_rows * breadth, local_filters)
    width_w = img_block.shape[2]
    blocks = []
    for weight_tap_row in range(3):
        for weight_tap_col in range(3):
            weight_window = img_block[
                weight_tap_row : weight_tap_row + pair_rows,
                weight_tap_col : weight_tap_col + breadth,
            ].reshape(pair_rows * breadth, width_w)
            blocks.append(
                lax.dot_general(
                    weight_window,
                    grad_flat,
                    (((0,), (0,)), ((), ())),
                    preferred_element_type=jnp.float32,
                )
            )
    stacked = jnp.stack(blocks).reshape(3, 3, width_w, local_filters)
    grad_weight = lax.psum_scatter(
        stacked.astype(jnp.bfloat16), "hi", scatter_dimension=2, tiled=True
    ).astype(jnp.float32)

    grad_rimmed = with_halo(grad_conv)
    input_term = conv(grad_rimmed, weight[::-1, ::-1], "HWOI")
    split = input_term.astype(jnp.bfloat16).reshape(height, breadth, chans, all_chans // chans)
    received = lax.all_to_all(split, "chan", split_axis=2, concat_axis=2, tiled=True)
    grad_input = jnp.sum(received.astype(jnp.float32), axis=2).astype(jnp.bfloat16)
    return (normed, grad_input, grad_weight)


def solution(mesh):
    slabs = mesh.shape["slab"]
    chans = mesh.shape["chan"]
    split_mesh = Mesh(mesh.devices.reshape(slabs // 2, 2, chans), ("hi", "lo", "chan"))
    return jax.shard_map(
        on_device,
        mesh=split_mesh,
        in_specs=(P(SLAB, None, "chan"), P(None, None, None, "chan"), P(SLAB, "chan", None)),
        out_specs=(P(SLAB, "chan", None), P(SLAB, None, "chan"), P(None, None, SLAB, "chan")),
        check_vma=False,
    )
```

```python
import jax
import jax.numpy as jnp
from jax import lax
from jax.sharding import Mesh
from jax.sharding import PartitionSpec as P

SLAB = ("hi", "lo")


def shift_rows(rows, upward):
    count = lax.axis_size(SLAB)
    if upward:
        pairs = [((i + 1), i) for i in range(count - 1)]
    else:
        pairs = [(i, i + 1) for i in range(count - 1)]
    return lax.ppermute(rows, SLAB, pairs)


def shift_sum(z):
    breadth = z.shape[-3]
    widths = [(0, 0)] * (z.ndim - 3) + [(1, 1), (0, 0), (0, 0)]
    zp = jnp.pad(z, widths)
    return zp[..., 0:breadth, 0, :] + zp[..., 1 : breadth + 1, 1, :] + zp[..., 2 : breadth + 2, 2, :]


def on_device(image, weight, grad_out):
    height = image.shape[0]
    breadth = image.shape[1]
    local_chans = image.shape[2]
    all_chans = weight.shape[2]
    local_filters = weight.shape[3]
    chans = lax.axis_size("chan")
    all_filters = local_filters * chans
    n_hi = lax.axis_size("hi")
    n_lo = lax.axis_size("lo")
    lo = lax.axis_index("lo")
    piece = all_chans // (n_hi * n_lo)
    per_chan = local_chans // (n_lo * piece)

    grad_filters = lax.all_to_all(grad_out, "chan", split_axis=2, concat_axis=1, tiled=True)
    gathered = lax.all_gather(image, "chan", axis=2, tiled=True)

    by_row = jnp.transpose(weight, (0, 2, 1, 3)).reshape(3, all_chans, 3 * local_filters)

    def taps(rows, a):
        count = rows.shape[0]
        flat = rows.reshape(count * breadth, all_chans)
        out = jnp.dot(flat, by_row[a], preferred_element_type=jnp.float32)
        return out.reshape(count, breadth, 3, local_filters)

    to_next = lax.ppermute(shift_sum(taps(gathered[-1:], 0)), SLAB, [(i, i + 1) for i in range(lax.axis_size(SLAB) - 1)])
    to_prev = lax.ppermute(shift_sum(taps(gathered[:1], 2)), SLAB, [(i + 1, i) for i in range(lax.axis_size(SLAB) - 1)])

    def local_subset(x, which):
        shaped = x.reshape(x.shape[0], x.shape[1], per_chan, n_lo, piece)
        taken = lax.dynamic_index_in_dim(shaped, which, axis=3, keepdims=False)
        return taken.reshape(x.shape[0], x.shape[1], per_chan * piece)

    raw6 = jnp.concatenate(
        [shift_rows(image[-1:], upward=False), image, shift_rows(image[:1], upward=True)], axis=0
    )
    send_rows = lax.dynamic_slice_in_dim(raw6, 2 * lo, height, axis=0)
    sent_img = lax.ppermute(local_subset(send_rows, 1 - lo), "lo", [(0, 1), (1, 0)])
    own_img = local_subset(raw6, lo)
    block_piece = lax.dynamic_slice_in_dim(
        jnp.concatenate([sent_img, own_img, sent_img], axis=0), height * (1 - lo), 2 * height + 2, axis=0
    )
    img_block = lax.all_gather(block_piece, "chan", axis=2, tiled=True)

    interior = taps(gathered, 1)
    interior = interior + jnp.pad(taps(gathered[:-1], 0), ((1, 0), (0, 0), (0, 0), (0, 0)))
    interior = interior + jnp.pad(taps(gathered[1:], 2), ((0, 1), (0, 0), (0, 0), (0, 0)))
    conv_sum = shift_sum(interior)
    conv_sum = conv_sum + jnp.concatenate(
        [to_next, jnp.zeros((height - 2, breadth, local_filters), jnp.float32), to_prev], axis=0
    )
    conv_out = conv_sum.astype(jnp.bfloat16)

    conv_wide = conv_out.astype(jnp.float32)
    upstream = grad_filters.astype(jnp.float32)
    partial = jnp.stack(
        [jnp.sum(conv_wide * conv_wide, axis=-1), jnp.sum(upstream * conv_wide, axis=-1)], axis=-1
    )
    totals = lax.psum(partial, "chan")
    inverse_rms = lax.rsqrt(totals[..., 0:1] / all_filters + 1e-06)
    mean_gu = inverse_rms * (totals[..., 1:2] / all_filters)
    unit = conv_wide * inverse_rms
    normed_filters = unit.astype(jnp.bfloat16)
    grad_conv = (inverse_rms * (upstream - unit * mean_gu)).astype(jnp.bfloat16)
    normed = lax.all_to_all(normed_filters, "chan", split_axis=1, concat_axis=2, tiled=True)

    sent_grad = lax.ppermute(grad_conv, "lo", [(0, 1), (1, 0)])
    img_block = jnp.pad(img_block, ((0, 0), (1, 1), (0, 0)))
    grad_block = lax.dynamic_slice_in_dim(
        jnp.concatenate([sent_grad, grad_conv, sent_grad], axis=0), height * (1 - lo), 2 * height, axis=0
    )
    pair_rows = 2 * height
    grad_flat = grad_block.reshape(pair_rows * breadth, local_filters)
    width_w = img_block.shape[2]
    blocks = []
    for weight_tap_row in range(3):
        for weight_tap_col in range(3):
            weight_window = img_block[
                weight_tap_row : weight_tap_row + pair_rows,
                weight_tap_col : weight_tap_col + breadth,
            ].reshape(pair_rows * breadth, width_w)
            blocks.append(
                lax.dot_general(
                    weight_window,
                    grad_flat,
                    (((0,), (0,)), ((), ())),
                    preferred_element_type=jnp.float32,
                )
            )
    stacked = jnp.stack(blocks).reshape(3, 3, width_w, local_filters)
    grad_weight = lax.psum_scatter(
        stacked.astype(jnp.bfloat16), "hi", scatter_dimension=2, tiled=True
    ).astype(jnp.float32)

    grad_rimmed = jnp.concatenate(
        [shift_rows(grad_conv[-1:], upward=False), grad_conv, shift_rows(grad_conv[:1], upward=True)], axis=0
    )
    grad_padded = jnp.pad(grad_rimmed, ((0, 0), (1, 1), (0, 0)))
    columns = jnp.concatenate(
        [
            grad_padded[a : a + height, b : b + breadth]
            for a in range(3)
            for b in range(3)
        ],
        axis=-1,
    ).reshape(height * breadth, 9 * local_filters)
    flipped = jnp.transpose(weight[::-1, ::-1], (0, 1, 3, 2)).reshape(9 * local_filters, all_chans)
    input_term = jnp.dot(columns, flipped, preferred_element_type=jnp.float32)
    split = input_term.astype(jnp.bfloat16).reshape(height, breadth, chans, all_chans // chans)
    received = lax.all_to_all(split, "chan", split_axis=2, concat_axis=2, tiled=True)
    grad_input = jnp.sum(received.astype(jnp.float32), axis=2).astype(jnp.bfloat16)
    return (normed, grad_input, grad_weight)


def solution(mesh):
    slabs = mesh.shape["slab"]
    chans = mesh.shape["chan"]
    split_mesh = Mesh(mesh.devices.reshape(slabs // 2, 2, chans), ("hi", "lo", "chan"))
    return jax.shard_map(
        on_device,
        mesh=split_mesh,
        in_specs=(P(SLAB, None, "chan"), P(None, None, None, "chan"), P(SLAB, "chan", None)),
        out_specs=(P(SLAB, "chan", None), P(SLAB, None, "chan"), P(None, None, SLAB, "chan")),
        check_vma=False,
    )
```

```python
import jax
import jax.numpy as jnp
from jax import lax
from jax.sharding import Mesh
from jax.sharding import PartitionSpec as P

SLAB = ("hi", "lo")


def shift_rows(rows, upward):
    count = lax.axis_size(SLAB)
    if upward:
        pairs = [((i + 1), i) for i in range(count - 1)]
    else:
        pairs = [(i, i + 1) for i in range(count - 1)]
    return lax.ppermute(rows, SLAB, pairs)


def shift_sum(z):
    breadth = z.shape[-3]
    widths = [(0, 0)] * (z.ndim - 3) + [(1, 1), (0, 0), (0, 0)]
    zp = jnp.pad(z, widths)
    return zp[..., 0:breadth, 0, :] + zp[..., 1 : breadth + 1, 1, :] + zp[..., 2 : breadth + 2, 2, :]


def on_device(image, weight, grad_out):
    height = image.shape[0]
    breadth = image.shape[1]
    local_chans = image.shape[2]
    all_chans = weight.shape[2]
    local_filters = weight.shape[3]
    chans = lax.axis_size("chan")
    all_filters = local_filters * chans
    n_hi = lax.axis_size("hi")
    n_lo = lax.axis_size("lo")
    lo = lax.axis_index("lo")
    piece = all_chans // (n_hi * n_lo)
    per_chan = local_chans // (n_lo * piece)

    grad_filters = lax.all_to_all(grad_out, "chan", split_axis=2, concat_axis=1, tiled=True)
    gathered = lax.all_gather(image, "chan", axis=2, tiled=True)

    by_row = jnp.transpose(weight, (0, 2, 1, 3)).reshape(3, all_chans, 3 * local_filters)

    def taps(rows, a):
        count = rows.shape[0]
        flat = rows.reshape(count * breadth, all_chans)
        out = jnp.dot(flat, by_row[a], preferred_element_type=jnp.float32)
        return out.reshape(count, breadth, 3, local_filters)

    to_next = lax.ppermute(shift_sum(taps(gathered[-1:], 0)), SLAB, [(i, i + 1) for i in range(lax.axis_size(SLAB) - 1)])
    to_prev = lax.ppermute(shift_sum(taps(gathered[:1], 2)), SLAB, [(i + 1, i) for i in range(lax.axis_size(SLAB) - 1)])

    def local_subset(x, which):
        shaped = x.reshape(x.shape[0], x.shape[1], per_chan, n_lo, piece)
        taken = lax.dynamic_index_in_dim(shaped, which, axis=3, keepdims=False)
        return taken.reshape(x.shape[0], x.shape[1], per_chan * piece)

    raw6 = jnp.concatenate(
        [shift_rows(image[-1:], upward=False), image, shift_rows(image[:1], upward=True)], axis=0
    )
    send_rows = lax.dynamic_slice_in_dim(raw6, 2 * lo, height, axis=0)
    sent_img = lax.ppermute(local_subset(send_rows, 1 - lo), "lo", [(0, 1), (1, 0)])
    own_img = local_subset(raw6, lo)
    block_piece = lax.dynamic_slice_in_dim(
        jnp.concatenate([sent_img, own_img, sent_img], axis=0), height * (1 - lo), 2 * height + 2, axis=0
    )
    img_block = lax.all_gather(block_piece, "chan", axis=2, tiled=True)

    interior = taps(gathered, 1)
    interior = interior + jnp.pad(taps(gathered[:-1], 0), ((1, 0), (0, 0), (0, 0), (0, 0)))
    interior = interior + jnp.pad(taps(gathered[1:], 2), ((0, 1), (0, 0), (0, 0), (0, 0)))
    conv_sum = shift_sum(interior)
    conv_sum = conv_sum + jnp.concatenate(
        [to_next, jnp.zeros((height - 2, breadth, local_filters), jnp.float32), to_prev], axis=0
    )
    conv_out = conv_sum.astype(jnp.bfloat16)

    conv_wide = conv_out.astype(jnp.float32)
    upstream = grad_filters.astype(jnp.float32)
    partial = jnp.stack(
        [jnp.sum(conv_wide * conv_wide, axis=-1), jnp.sum(upstream * conv_wide, axis=-1)], axis=-1
    )
    totals = lax.psum(partial, "chan")
    inverse_rms = lax.rsqrt(totals[..., 0:1] / all_filters + 1e-06)
    mean_gu = inverse_rms * (totals[..., 1:2] / all_filters)
    unit = conv_wide * inverse_rms
    normed_filters = unit.astype(jnp.bfloat16)
    grad_conv = (inverse_rms * (upstream - unit * mean_gu)).astype(jnp.bfloat16)
    normed = lax.all_to_all(normed_filters, "chan", split_axis=1, concat_axis=2, tiled=True)

    sent_grad = lax.ppermute(grad_conv, "lo", [(0, 1), (1, 0)])
    img_block = jnp.pad(img_block, ((0, 0), (1, 1), (0, 0)))
    width_w = img_block.shape[2]

    def pair_part(grad_rows, first_row):
        flat = grad_rows.reshape(height * breadth, local_filters)
        blocks = []
        for weight_tap_row in range(3):
            rows = lax.dynamic_slice_in_dim(img_block, first_row + weight_tap_row, height, axis=0)
            for weight_tap_col in range(3):
                weight_window = rows[:, weight_tap_col : weight_tap_col + breadth].reshape(height * breadth, width_w)
                blocks.append(
                    lax.dot_general(
                        weight_window,
                        flat,
                        (((0,), (0,)), ((), ())),
                        preferred_element_type=jnp.float32,
                    )
                )
        return jnp.stack(blocks)

    own_part = pair_part(grad_conv, height * lo)

    grad_rimmed = jnp.concatenate(
        [shift_rows(grad_conv[-1:], upward=False), grad_conv, shift_rows(grad_conv[:1], upward=True)], axis=0
    )
    grad_padded = jnp.pad(grad_rimmed, ((0, 0), (1, 1), (0, 0)))
    columns = jnp.concatenate(
        [
            grad_padded[2 - a : 2 - a + height, 2 - b : 2 - b + breadth]
            for a in range(3)
            for b in range(3)
        ],
        axis=-1,
    ).reshape(height * breadth, 9 * local_filters)
    by_filter = jnp.transpose(weight, (0, 1, 3, 2)).reshape(9 * local_filters, all_chans)
    input_term = jnp.dot(columns, by_filter, preferred_element_type=jnp.float32)
    split = input_term.astype(jnp.bfloat16).reshape(height, breadth, chans, all_chans // chans)
    received = lax.all_to_all(split, "chan", split_axis=2, concat_axis=2, tiled=True)
    grad_input = jnp.sum(received.astype(jnp.float32), axis=2).astype(jnp.bfloat16)
    sent_grad, _, own_part = lax.optimization_barrier((sent_grad, split, own_part))

    stacked = (own_part + pair_part(sent_grad, height * (1 - lo))).reshape(3, 3, width_w, local_filters)
    grad_weight = lax.psum_scatter(
        stacked.astype(jnp.bfloat16), "hi", scatter_dimension=2, tiled=True
    ).astype(jnp.float32)
    return (normed, grad_input, grad_weight)


def solution(mesh):
    slabs = mesh.shape["slab"]
    chans = mesh.shape["chan"]
    split_mesh = Mesh(mesh.devices.reshape(slabs // 2, 2, chans), ("hi", "lo", "chan"))
    return jax.shard_map(
        on_device,
        mesh=split_mesh,
        in_specs=(P(SLAB, None, "chan"), P(None, None, None, "chan"), P(SLAB, "chan", None)),
        out_specs=(P(SLAB, "chan", None), P(SLAB, None, "chan"), P(None, None, SLAB, "chan")),
        check_vma=False,
    )
```

```python
import jax
import jax.numpy as jnp
from jax import lax
from jax.sharding import Mesh
from jax.sharding import PartitionSpec as P

SLAB = ("hi", "lo")


def shift_rows(rows, upward):
    count = lax.axis_size(SLAB)
    if upward:
        pairs = [((i + 1), i) for i in range(count - 1)]
    else:
        pairs = [(i, i + 1) for i in range(count - 1)]
    return lax.ppermute(rows, SLAB, pairs)


def shift_sum(z):
    breadth = z.shape[-3]
    widths = [(0, 0)] * (z.ndim - 3) + [(1, 1), (0, 0), (0, 0)]
    zp = jnp.pad(z, widths)
    return zp[..., 0:breadth, 0, :] + zp[..., 1 : breadth + 1, 1, :] + zp[..., 2 : breadth + 2, 2, :]


def on_device(image, weight, grad_out):
    height = image.shape[0]
    breadth = image.shape[1]
    local_chans = image.shape[2]
    all_chans = weight.shape[2]
    local_filters = weight.shape[3]
    chans = lax.axis_size("chan")
    all_filters = local_filters * chans
    n_hi = lax.axis_size("hi")
    n_lo = lax.axis_size("lo")
    lo = lax.axis_index("lo")
    piece = all_chans // (n_hi * n_lo)
    per_chan = local_chans // (n_lo * piece)

    grad_filters = lax.all_to_all(grad_out, "chan", split_axis=2, concat_axis=1, tiled=True)
    gathered = lax.all_gather(image, "chan", axis=2, tiled=True)

    by_row = jnp.transpose(weight, (0, 2, 1, 3)).reshape(3, all_chans, 3 * local_filters)

    def taps(rows, a):
        count = rows.shape[0]
        flat = rows.reshape(count * breadth, all_chans)
        out = jnp.dot(flat, by_row[a], preferred_element_type=jnp.float32)
        return out.reshape(count, breadth, 3, local_filters)

    to_next = lax.ppermute(shift_sum(taps(gathered[-1:], 0)), SLAB, [(i, i + 1) for i in range(lax.axis_size(SLAB) - 1)])
    to_prev = lax.ppermute(shift_sum(taps(gathered[:1], 2)), SLAB, [(i + 1, i) for i in range(lax.axis_size(SLAB) - 1)])

    def local_subset(x, which):
        shaped = x.reshape(x.shape[0], x.shape[1], per_chan, n_lo, piece)
        taken = lax.dynamic_index_in_dim(shaped, which, axis=3, keepdims=False)
        return taken.reshape(x.shape[0], x.shape[1], per_chan * piece)

    raw6 = jnp.concatenate(
        [shift_rows(image[-1:], upward=False), image, shift_rows(image[:1], upward=True)], axis=0
    )
    send_rows = lax.dynamic_slice_in_dim(raw6, 2 * lo, height, axis=0)
    sent_img = lax.ppermute(local_subset(send_rows, 1 - lo), "lo", [(0, 1), (1, 0)])
    own_img = local_subset(raw6, lo)
    block_piece = lax.dynamic_slice_in_dim(
        jnp.concatenate([sent_img, own_img, sent_img], axis=0), height * (1 - lo), 2 * height + 2, axis=0
    )
    img_block = lax.all_gather(block_piece, "chan", axis=2, tiled=True)

    interior = taps(gathered, 1)
    interior = interior + jnp.pad(taps(gathered[:-1], 0), ((1, 0), (0, 0), (0, 0), (0, 0)))
    interior = interior + jnp.pad(taps(gathered[1:], 2), ((0, 1), (0, 0), (0, 0), (0, 0)))
    conv_sum = shift_sum(interior)
    conv_sum = conv_sum + jnp.concatenate(
        [to_next, jnp.zeros((height - 2, breadth, local_filters), jnp.float32), to_prev], axis=0
    )
    conv_out = conv_sum.astype(jnp.bfloat16)

    conv_wide = conv_out.astype(jnp.float32)
    upstream = grad_filters.astype(jnp.float32)
    partial = jnp.stack(
        [jnp.sum(conv_wide * conv_wide, axis=-1), jnp.sum(upstream * conv_wide, axis=-1)], axis=-1
    )
    totals = lax.psum(partial, "chan")
    inverse_rms = lax.rsqrt(totals[..., 0:1] / all_filters + 1e-06)
    mean_gu = inverse_rms * (totals[..., 1:2] / all_filters)
    unit = conv_wide * inverse_rms
    normed_filters = unit.astype(jnp.bfloat16)
    grad_conv = (inverse_rms * (upstream - unit * mean_gu)).astype(jnp.bfloat16)

    sent_grad = lax.ppermute(grad_conv, "lo", [(0, 1), (1, 0)])
    img_block = jnp.pad(img_block, ((0, 0), (1, 1), (0, 0)))
    width_w = img_block.shape[2]

    def pair_part(grad_rows, first_row):
        flat = grad_rows.reshape(height * breadth, local_filters)
        blocks = []
        for weight_tap_row in range(3):
            rows = lax.dynamic_slice_in_dim(img_block, first_row + weight_tap_row, height, axis=0)
            for weight_tap_col in range(3):
                weight_window = rows[:, weight_tap_col : weight_tap_col + breadth].reshape(height * breadth, width_w)
                blocks.append(
                    lax.dot_general(
                        weight_window,
                        flat,
                        (((0,), (0,)), ((), ())),
                        preferred_element_type=jnp.float32,
                    )
                )
        return jnp.stack(blocks)

    own_part = pair_part(grad_conv, height * lo)
    sent_grad, own_part = lax.optimization_barrier((sent_grad, own_part))
    stacked = (own_part + pair_part(sent_grad, height * (1 - lo))).astype(jnp.bfloat16)
    grad_weight = lax.psum_scatter(
        stacked.reshape(3, 3, width_w, local_filters), "hi", scatter_dimension=2, tiled=True
    ).astype(jnp.float32)

    grad_late, normed_late, _ = lax.optimization_barrier((grad_conv, normed_filters, stacked))
    normed = lax.all_to_all(normed_late, "chan", split_axis=1, concat_axis=2, tiled=True)

    grad_rimmed = jnp.concatenate(
        [shift_rows(grad_late[-1:], upward=False), grad_late, shift_rows(grad_late[:1], upward=True)], axis=0
    )
    grad_padded = jnp.pad(grad_rimmed, ((0, 0), (1, 1), (0, 0)))
    columns = jnp.concatenate(
        [
            grad_padded[2 - a : 2 - a + height, 2 - b : 2 - b + breadth]
            for a in range(3)
            for b in range(3)
        ],
        axis=-1,
    ).reshape(height * breadth, 9 * local_filters)
    by_filter = jnp.transpose(weight, (0, 1, 3, 2)).reshape(9 * local_filters, all_chans)
    input_term = jnp.dot(columns, by_filter, preferred_element_type=jnp.float32)
    split = input_term.astype(jnp.bfloat16).reshape(height, breadth, chans, all_chans // chans)
    received = lax.all_to_all(split, "chan", split_axis=2, concat_axis=2, tiled=True)
    grad_input = jnp.sum(received.astype(jnp.float32), axis=2).astype(jnp.bfloat16)
    return (normed, grad_input, grad_weight)


def solution(mesh):
    slabs = mesh.shape["slab"]
    chans = mesh.shape["chan"]
    split_mesh = Mesh(mesh.devices.reshape(slabs // 2, 2, chans), ("hi", "lo", "chan"))
    return jax.shard_map(
        on_device,
        mesh=split_mesh,
        in_specs=(P(SLAB, None, "chan"), P(None, None, None, "chan"), P(SLAB, "chan", None)),
        out_specs=(P(SLAB, "chan", None), P(SLAB, None, "chan"), P(None, None, SLAB, "chan")),
        check_vma=False,
    )
```

```python
import jax
import jax.numpy as jnp
from jax import lax
from jax.sharding import Mesh
from jax.sharding import PartitionSpec as P

SLAB = ("hi", "lo")


def shift_rows(rows, upward):
    count = lax.axis_size(SLAB)
    if upward:
        pairs = [((i + 1), i) for i in range(count - 1)]
    else:
        pairs = [(i, i + 1) for i in range(count - 1)]
    return lax.ppermute(rows, SLAB, pairs)


def shift_sum(z):
    breadth = z.shape[-3]
    widths = [(0, 0)] * (z.ndim - 3) + [(1, 1), (0, 0), (0, 0)]
    zp = jnp.pad(z, widths)
    return zp[..., 0:breadth, 0, :] + zp[..., 1 : breadth + 1, 1, :] + zp[..., 2 : breadth + 2, 2, :]


def on_device(image, weight, grad_out):
    height = image.shape[0]
    breadth = image.shape[1]
    local_chans = image.shape[2]
    all_chans = weight.shape[2]
    local_filters = weight.shape[3]
    chans = lax.axis_size("chan")
    all_filters = local_filters * chans
    n_hi = lax.axis_size("hi")
    n_lo = lax.axis_size("lo")
    lo = lax.axis_index("lo")
    piece = all_chans // (n_hi * n_lo)
    per_chan = local_chans // (n_lo * piece)

    grad_filters = lax.all_to_all(grad_out, "chan", split_axis=2, concat_axis=1, tiled=True)
    gathered = lax.all_gather(image, "chan", axis=2, tiled=True)

    by_row = jnp.transpose(weight, (0, 2, 1, 3)).reshape(3, all_chans, 3 * local_filters)

    def taps(rows, a):
        count = rows.shape[0]
        flat = rows.reshape(count * breadth, all_chans)
        out = jnp.dot(flat, by_row[a], preferred_element_type=jnp.float32)
        return out.reshape(count, breadth, 3, local_filters)

    to_next = lax.ppermute(shift_sum(taps(gathered[-1:], 0)), SLAB, [(i, i + 1) for i in range(lax.axis_size(SLAB) - 1)])
    to_prev = lax.ppermute(shift_sum(taps(gathered[:1], 2)), SLAB, [(i + 1, i) for i in range(lax.axis_size(SLAB) - 1)])

    def local_subset(x, which):
        shaped = x.reshape(x.shape[0], x.shape[1], per_chan, n_lo, piece)
        taken = lax.dynamic_index_in_dim(shaped, which, axis=3, keepdims=False)
        return taken.reshape(x.shape[0], x.shape[1], per_chan * piece)

    raw6 = jnp.concatenate(
        [shift_rows(image[-1:], upward=False), image, shift_rows(image[:1], upward=True)], axis=0
    )
    send_rows = lax.dynamic_slice_in_dim(raw6, 2 * lo, height, axis=0)
    sent_img = lax.ppermute(local_subset(send_rows, 1 - lo), "lo", [(0, 1), (1, 0)])
    own_img = local_subset(raw6, lo)
    block_piece = lax.dynamic_slice_in_dim(
        jnp.concatenate([sent_img, own_img, sent_img], axis=0), height * (1 - lo), 2 * height + 2, axis=0
    )
    img_block = lax.all_gather(block_piece, "chan", axis=2, tiled=True)

    interior = taps(gathered, 1)
    interior = interior + jnp.pad(taps(gathered[:-1], 0), ((1, 0), (0, 0), (0, 0), (0, 0)))
    interior = interior + jnp.pad(taps(gathered[1:], 2), ((0, 1), (0, 0), (0, 0), (0, 0)))
    conv_sum = shift_sum(interior)
    conv_sum = conv_sum + jnp.concatenate(
        [to_next, jnp.zeros((height - 2, breadth, local_filters), jnp.float32), to_prev], axis=0
    )
    conv_out = conv_sum.astype(jnp.bfloat16)

    conv_wide = conv_out.astype(jnp.float32)
    upstream = grad_filters.astype(jnp.float32)
    partial = jnp.stack(
        [jnp.sum(conv_wide * conv_wide, axis=-1), jnp.sum(upstream * conv_wide, axis=-1)], axis=-1
    )
    totals = lax.psum(partial, "chan")
    inverse_rms = lax.rsqrt(totals[..., 0:1] / all_filters + 1e-06)
    mean_gu = inverse_rms * (totals[..., 1:2] / all_filters)
    unit = conv_wide * inverse_rms
    normed_filters = unit.astype(jnp.bfloat16)
    grad_conv = (inverse_rms * (upstream - unit * mean_gu)).astype(jnp.bfloat16)
    normed = lax.all_to_all(normed_filters, "chan", split_axis=1, concat_axis=2, tiled=True)

    sent_grad = lax.ppermute(grad_conv, "lo", [(0, 1), (1, 0)])
    img_block = jnp.pad(img_block, ((0, 0), (1, 1), (0, 0)))
    grad_block = lax.dynamic_slice_in_dim(
        jnp.concatenate([sent_grad, grad_conv, sent_grad], axis=0), height * (1 - lo), 2 * height, axis=0
    )
    pair_rows = 2 * height
    grad_flat = grad_block.reshape(pair_rows * breadth, local_filters)
    width_w = img_block.shape[2]
    blocks = []
    for weight_tap_row in range(3):
        for weight_tap_col in range(3):
            weight_window = img_block[
                weight_tap_row : weight_tap_row + pair_rows,
                weight_tap_col : weight_tap_col + breadth,
            ].reshape(pair_rows * breadth, width_w)
            blocks.append(
                lax.dot_general(
                    weight_window,
                    grad_flat,
                    (((0,), (0,)), ((), ())),
                    preferred_element_type=jnp.float32,
                )
            )
    stacked = jnp.stack(blocks).reshape(3, 3, width_w, local_filters)
    grad_weight = lax.psum_scatter(
        stacked.astype(jnp.bfloat16), "hi", scatter_dimension=2, tiled=True
    ).astype(jnp.float32)

    grad_rimmed = jnp.concatenate(
        [shift_rows(grad_conv[-1:], upward=False), grad_conv, shift_rows(grad_conv[:1], upward=True)], axis=0
    )
    grad_padded = jnp.pad(grad_rimmed, ((0, 0), (1, 1), (0, 0)))
    columns = jnp.concatenate(
        [
            grad_padded[2 - a : 2 - a + height, 2 - b : 2 - b + breadth]
            for a in range(3)
            for b in range(3)
        ],
        axis=-1,
    ).reshape(height * breadth, 9 * local_filters)
    by_filter = jnp.transpose(weight, (0, 1, 3, 2)).reshape(9 * local_filters, all_chans)
    input_term = jnp.dot(columns, by_filter, preferred_element_type=jnp.float32)
    split = input_term.astype(jnp.bfloat16).reshape(height, breadth, chans, all_chans // chans)
    received = lax.all_to_all(split, "chan", split_axis=2, concat_axis=2, tiled=True)
    grad_input = jnp.sum(received.astype(jnp.float32), axis=2).astype(jnp.bfloat16)
    return (normed, grad_input, grad_weight)


def solution(mesh):
    slabs = mesh.shape["slab"]
    chans = mesh.shape["chan"]
    split_mesh = Mesh(mesh.devices.reshape(slabs // 2, 2, chans), ("hi", "lo", "chan"))
    return jax.shard_map(
        on_device,
        mesh=split_mesh,
        in_specs=(P(SLAB, None, "chan"), P(None, None, None, "chan"), P(SLAB, "chan", None)),
        out_specs=(P(SLAB, "chan", None), P(SLAB, None, "chan"), P(None, None, SLAB, "chan")),
        check_vma=False,
    )
```

```python
import jax
import jax.numpy as jnp
from jax import lax
from jax.sharding import Mesh
from jax.sharding import PartitionSpec as P

SLAB = ("hi", "lo")


def shift_rows(rows, upward):
    count = lax.axis_size(SLAB)
    if upward:
        pairs = [((i + 1), i) for i in range(count - 1)]
    else:
        pairs = [(i, i + 1) for i in range(count - 1)]
    return lax.ppermute(rows, SLAB, pairs)


def shift_sum(z):
    breadth = z.shape[-3]
    widths = [(0, 0)] * (z.ndim - 3) + [(1, 1), (0, 0), (0, 0)]
    zp = jnp.pad(z, widths)
    return zp[..., 0:breadth, 0, :] + zp[..., 1 : breadth + 1, 1, :] + zp[..., 2 : breadth + 2, 2, :]


def on_device(image, weight, grad_out):
    height = image.shape[0]
    breadth = image.shape[1]
    local_chans = image.shape[2]
    all_chans = weight.shape[2]
    local_filters = weight.shape[3]
    chans = lax.axis_size("chan")
    all_filters = local_filters * chans
    n_hi = lax.axis_size("hi")
    n_lo = lax.axis_size("lo")
    lo = lax.axis_index("lo")
    piece = all_chans // (n_hi * n_lo)
    per_chan = local_chans // (n_lo * piece)

    grad_filters = lax.all_to_all(grad_out, "chan", split_axis=2, concat_axis=1, tiled=True)
    gathered = lax.all_gather(image, "chan", axis=2, tiled=True)

    by_row = jnp.transpose(weight, (0, 2, 1, 3)).reshape(3, all_chans, 3 * local_filters)

    def taps(rows, a):
        count = rows.shape[0]
        flat = rows.reshape(count * breadth, all_chans)
        out = jnp.dot(flat, by_row[a], preferred_element_type=jnp.float32)
        return out.reshape(count, breadth, 3, local_filters)

    to_next = lax.ppermute(shift_sum(taps(gathered[-1:], 0)), SLAB, [(i, i + 1) for i in range(lax.axis_size(SLAB) - 1)])
    to_prev = lax.ppermute(shift_sum(taps(gathered[:1], 2)), SLAB, [(i + 1, i) for i in range(lax.axis_size(SLAB) - 1)])

    def local_subset(x, which):
        shaped = x.reshape(x.shape[0], x.shape[1], per_chan, n_lo, piece)
        taken = lax.dynamic_index_in_dim(shaped, which, axis=3, keepdims=False)
        return taken.reshape(x.shape[0], x.shape[1], per_chan * piece)

    raw6 = jnp.concatenate(
        [shift_rows(image[-1:], upward=False), image, shift_rows(image[:1], upward=True)], axis=0
    )
    send_rows = lax.dynamic_slice_in_dim(raw6, 2 * lo, height, axis=0)
    sent_img = lax.ppermute(local_subset(send_rows, 1 - lo), "lo", [(0, 1), (1, 0)])
    own_img = local_subset(raw6, lo)
    block_piece = lax.dynamic_slice_in_dim(
        jnp.concatenate([sent_img, own_img, sent_img], axis=0), height * (1 - lo), 2 * height + 2, axis=0
    )
    img_block = lax.all_gather(block_piece, "chan", axis=2, tiled=True)

    interior = taps(gathered, 1)
    interior = interior + jnp.pad(taps(gathered[:-1], 0), ((1, 0), (0, 0), (0, 0), (0, 0)))
    interior = interior + jnp.pad(taps(gathered[1:], 2), ((0, 1), (0, 0), (0, 0), (0, 0)))
    conv_sum = shift_sum(interior)
    conv_sum = conv_sum + jnp.concatenate(
        [to_next, jnp.zeros((height - 2, breadth, local_filters), jnp.float32), to_prev], axis=0
    )
    conv_out = conv_sum.astype(jnp.bfloat16)

    conv_wide = conv_out.astype(jnp.float32)
    upstream = grad_filters.astype(jnp.float32)
    partial = jnp.stack(
        [jnp.sum(conv_wide * conv_wide, axis=-1), jnp.sum(upstream * conv_wide, axis=-1)], axis=-1
    )
    totals = lax.psum(partial, "chan")
    inverse_rms = lax.rsqrt(totals[..., 0:1] / all_filters + 1e-06)
    mean_gu = inverse_rms * (totals[..., 1:2] / all_filters)
    unit = conv_wide * inverse_rms
    normed_filters = unit.astype(jnp.bfloat16)
    grad_conv = (inverse_rms * (upstream - unit * mean_gu)).astype(jnp.bfloat16)
    normed = lax.all_to_all(normed_filters, "chan", split_axis=1, concat_axis=2, tiled=True)

    sent_grad = lax.ppermute(grad_conv, "lo", [(0, 1), (1, 0)])
    width_w = img_block.shape[2]

    def pair_part(grad_rows, first_row):
        grad_cols = jnp.pad(grad_rows, ((0, 0), (1, 1), (0, 0)))
        shifted = jnp.stack([grad_cols[:, 2 - b : 2 - b + breadth] for b in range(3)], axis=2)
        shifted = shifted.reshape(height * breadth, 3 * local_filters)
        rows = [
            lax.dynamic_slice_in_dim(img_block, first_row + a, height, axis=0).reshape(height * breadth, width_w)
            for a in range(3)
        ]
        return jnp.stack(
            [
                lax.dot_general(r, shifted, (((0,), (0,)), ((), ())), preferred_element_type=jnp.float32)
                for r in rows
            ]
        )

    own_part = pair_part(grad_conv, height * lo)
    sent_grad, own_part = lax.optimization_barrier((sent_grad, own_part))
    summed = own_part + pair_part(sent_grad, height * (1 - lo))
    stacked = jnp.transpose(summed.reshape(3, width_w, 3, local_filters), (0, 2, 1, 3))
    grad_weight = lax.psum_scatter(
        stacked.astype(jnp.bfloat16), "hi", scatter_dimension=2, tiled=True
    ).astype(jnp.float32)

    grad_rimmed = jnp.concatenate(
        [shift_rows(grad_conv[-1:], upward=False), grad_conv, shift_rows(grad_conv[:1], upward=True)], axis=0
    )
    grad_padded = jnp.pad(grad_rimmed, ((0, 0), (1, 1), (0, 0)))
    columns = jnp.concatenate(
        [
            grad_padded[2 - a : 2 - a + height, 2 - b : 2 - b + breadth]
            for a in range(3)
            for b in range(3)
        ],
        axis=-1,
    ).reshape(height * breadth, 9 * local_filters)
    by_filter = jnp.transpose(weight, (0, 1, 3, 2)).reshape(9 * local_filters, all_chans)
    input_term = jnp.dot(columns, by_filter, preferred_element_type=jnp.float32)
    split = input_term.astype(jnp.bfloat16).reshape(height, breadth, chans, all_chans // chans)
    received = lax.all_to_all(split, "chan", split_axis=2, concat_axis=2, tiled=True)
    grad_input = jnp.sum(received.astype(jnp.float32), axis=2).astype(jnp.bfloat16)
    return (normed, grad_input, grad_weight)


def solution(mesh):
    slabs = mesh.shape["slab"]
    chans = mesh.shape["chan"]
    split_mesh = Mesh(mesh.devices.reshape(slabs // 2, 2, chans), ("hi", "lo", "chan"))
    return jax.shard_map(
        on_device,
        mesh=split_mesh,
        in_specs=(P(SLAB, None, "chan"), P(None, None, None, "chan"), P(SLAB, "chan", None)),
        out_specs=(P(SLAB, "chan", None), P(SLAB, None, "chan"), P(None, None, SLAB, "chan")),
        check_vma=False,
    )
```

```python
import jax
import jax.numpy as jnp
from jax import lax
from jax.sharding import Mesh
from jax.sharding import PartitionSpec as P

SLAB = ("hi", "lo")


def shift_rows(rows, upward):
    count = lax.axis_size(SLAB)
    if upward:
        pairs = [((i + 1), i) for i in range(count - 1)]
    else:
        pairs = [(i, i + 1) for i in range(count - 1)]
    return lax.ppermute(rows, SLAB, pairs)


def shift_sum(z):
    breadth = z.shape[-3]
    widths = [(0, 0)] * (z.ndim - 3) + [(1, 1), (0, 0), (0, 0)]
    zp = jnp.pad(z, widths)
    return zp[..., 0:breadth, 0, :] + zp[..., 1 : breadth + 1, 1, :] + zp[..., 2 : breadth + 2, 2, :]


def on_device(image, weight, grad_out):
    height = image.shape[0]
    breadth = image.shape[1]
    local_chans = image.shape[2]
    all_chans = weight.shape[2]
    local_filters = weight.shape[3]
    chans = lax.axis_size("chan")
    all_filters = local_filters * chans
    n_hi = lax.axis_size("hi")
    n_lo = lax.axis_size("lo")
    lo = lax.axis_index("lo")
    piece = all_chans // (n_hi * n_lo)
    per_chan = local_chans // (n_lo * piece)

    grad_filters = lax.all_to_all(grad_out, "chan", split_axis=2, concat_axis=1, tiled=True)
    gathered = lax.all_gather(image, "chan", axis=2, tiled=True)

    by_row = jnp.transpose(weight, (0, 2, 1, 3)).reshape(3, all_chans, 3 * local_filters)

    def taps(rows, a):
        count = rows.shape[0]
        flat = rows.reshape(count * breadth, all_chans)
        out = jnp.dot(flat, by_row[a], preferred_element_type=jnp.float32)
        return out.reshape(count, breadth, 3, local_filters)

    to_next = lax.ppermute(shift_sum(taps(gathered[-1:], 0)), SLAB, [(i, i + 1) for i in range(lax.axis_size(SLAB) - 1)])
    to_prev = lax.ppermute(shift_sum(taps(gathered[:1], 2)), SLAB, [(i + 1, i) for i in range(lax.axis_size(SLAB) - 1)])

    def local_subset(x, which):
        shaped = x.reshape(x.shape[0], x.shape[1], per_chan, n_lo, piece)
        taken = lax.dynamic_index_in_dim(shaped, which, axis=3, keepdims=False)
        return taken.reshape(x.shape[0], x.shape[1], per_chan * piece)

    raw6 = jnp.concatenate(
        [shift_rows(image[-1:], upward=False), image, shift_rows(image[:1], upward=True)], axis=0
    )
    send_rows = lax.dynamic_slice_in_dim(raw6, 2 * lo, height, axis=0)
    sent_img = lax.ppermute(local_subset(send_rows, 1 - lo), "lo", [(0, 1), (1, 0)])
    own_img = local_subset(raw6, lo)
    block_piece = lax.dynamic_slice_in_dim(
        jnp.concatenate([sent_img, own_img, sent_img], axis=0), height * (1 - lo), 2 * height + 2, axis=0
    )
    img_block = lax.all_gather(block_piece, "chan", axis=2, tiled=True)

    interior = taps(gathered, 1)
    interior = interior + jnp.pad(taps(gathered[:-1], 0), ((1, 0), (0, 0), (0, 0), (0, 0)))
    interior = interior + jnp.pad(taps(gathered[1:], 2), ((0, 1), (0, 0), (0, 0), (0, 0)))
    conv_sum = shift_sum(interior)
    conv_sum = conv_sum + jnp.concatenate(
        [to_next, jnp.zeros((height - 2, breadth, local_filters), jnp.float32), to_prev], axis=0
    )
    conv_out = conv_sum.astype(jnp.bfloat16)

    conv_wide = conv_out.astype(jnp.float32)
    upstream = grad_filters.astype(jnp.float32)
    partial = jnp.stack(
        [jnp.sum(conv_wide * conv_wide, axis=-1), jnp.sum(upstream * conv_wide, axis=-1)], axis=-1
    )
    totals = lax.psum(partial, "chan")
    inverse_rms = lax.rsqrt(totals[..., 0:1] / all_filters + 1e-06)
    mean_gu = inverse_rms * (totals[..., 1:2] / all_filters)
    unit = conv_wide * inverse_rms
    normed_filters = unit.astype(jnp.bfloat16)
    grad_conv = (inverse_rms * (upstream - unit * mean_gu)).astype(jnp.bfloat16)
    normed = lax.all_to_all(normed_filters, "chan", split_axis=1, concat_axis=2, tiled=True)

    sent_grad = lax.ppermute(grad_conv, "lo", [(0, 1), (1, 0)])
    img_block = jnp.pad(img_block, ((0, 0), (1, 1), (0, 0)))
    width_w = img_block.shape[2]

    def pair_part(grad_rows, first_row):
        flat = grad_rows.reshape(height * breadth, local_filters)
        blocks = []
        for weight_tap_row in range(3):
            rows = lax.dynamic_slice_in_dim(img_block, first_row + weight_tap_row, height, axis=0)
            for weight_tap_col in range(3):
                weight_window = rows[:, weight_tap_col : weight_tap_col + breadth].reshape(height * breadth, width_w)
                blocks.append(
                    lax.dot_general(
                        weight_window,
                        flat,
                        (((0,), (0,)), ((), ())),
                        preferred_element_type=jnp.float32,
                    )
                )
        return jnp.stack(blocks)

    own_part = pair_part(grad_conv, height * lo)
    sent_grad, own_part = lax.optimization_barrier((sent_grad, own_part))
    stacked = (own_part + pair_part(sent_grad, height * (1 - lo))).reshape(3, 3, width_w, local_filters)
    grad_weight = lax.psum_scatter(
        stacked.astype(jnp.bfloat16), "hi", scatter_dimension=2, tiled=True
    ).astype(jnp.float32)

    grad_rimmed = jnp.concatenate(
        [shift_rows(grad_conv[-1:], upward=False), grad_conv, shift_rows(grad_conv[:1], upward=True)], axis=0
    )
    grad_padded = jnp.pad(grad_rimmed, ((0, 0), (1, 1), (0, 0)))
    columns = jnp.concatenate(
        [
            grad_padded[2 - a : 2 - a + height, 2 - b : 2 - b + breadth]
            for a in range(3)
            for b in range(3)
        ],
        axis=-1,
    ).reshape(height * breadth, 9 * local_filters)
    by_filter = jnp.transpose(weight, (0, 1, 3, 2)).reshape(9 * local_filters, all_chans)
    input_term = jnp.dot(columns, by_filter, preferred_element_type=jnp.float32)
    split = input_term.astype(jnp.bfloat16).reshape(height, breadth, chans, all_chans // chans)
    received = lax.all_to_all(split, "chan", split_axis=2, concat_axis=2, tiled=True)
    grad_input = jnp.sum(received.astype(jnp.float32), axis=2).astype(jnp.bfloat16)
    return (normed, grad_input, grad_weight)


def solution(mesh):
    slabs = mesh.shape["slab"]
    chans = mesh.shape["chan"]
    split_mesh = Mesh(mesh.devices.reshape(slabs // 2, 2, chans), ("hi", "lo", "chan"))
    return jax.shard_map(
        on_device,
        mesh=split_mesh,
        in_specs=(P(SLAB, None, "chan"), P(None, None, None, "chan"), P(SLAB, "chan", None)),
        out_specs=(P(SLAB, "chan", None), P(SLAB, None, "chan"), P(None, None, SLAB, "chan")),
        check_vma=False,
    )
```

```python
import jax
import jax.numpy as jnp
from jax import lax
from jax.sharding import Mesh
from jax.sharding import PartitionSpec as P

SLAB = ("hi", "lo")


def shift_rows(rows, upward):
    count = lax.axis_size(SLAB)
    if upward:
        pairs = [((i + 1), i) for i in range(count - 1)]
    else:
        pairs = [(i, i + 1) for i in range(count - 1)]
    return lax.ppermute(rows, SLAB, pairs)


def shift_sum(z):
    breadth = z.shape[-3]
    widths = [(0, 0)] * (z.ndim - 3) + [(1, 1), (0, 0), (0, 0)]
    zp = jnp.pad(z, widths)
    return zp[..., 0:breadth, 0, :] + zp[..., 1 : breadth + 1, 1, :] + zp[..., 2 : breadth + 2, 2, :]


def on_device(image, weight, grad_out):
    height = image.shape[0]
    breadth = image.shape[1]
    local_chans = image.shape[2]
    all_chans = weight.shape[2]
    local_filters = weight.shape[3]
    chans = lax.axis_size("chan")
    all_filters = local_filters * chans
    n_hi = lax.axis_size("hi")
    n_lo = lax.axis_size("lo")
    lo = lax.axis_index("lo")
    piece = all_chans // (n_hi * n_lo)
    per_chan = local_chans // (n_lo * piece)

    grad_filters = lax.all_to_all(grad_out, "chan", split_axis=2, concat_axis=1, tiled=True)
    gathered = lax.all_gather(image, "chan", axis=2, tiled=True)

    by_row = jnp.transpose(weight, (0, 2, 1, 3)).reshape(3, all_chans, 3 * local_filters)

    def taps(rows, a):
        count = rows.shape[0]
        flat = rows.reshape(count * breadth, all_chans)
        out = jnp.dot(flat, by_row[a], preferred_element_type=jnp.float32)
        return out.reshape(count, breadth, 3, local_filters)

    to_next = lax.ppermute(shift_sum(taps(gathered[-1:], 0)), SLAB, [(i, i + 1) for i in range(lax.axis_size(SLAB) - 1)])
    to_prev = lax.ppermute(shift_sum(taps(gathered[:1], 2)), SLAB, [(i + 1, i) for i in range(lax.axis_size(SLAB) - 1)])

    def local_subset(x, which):
        shaped = x.reshape(x.shape[0], x.shape[1], per_chan, n_lo, piece)
        taken = lax.dynamic_index_in_dim(shaped, which, axis=3, keepdims=False)
        return taken.reshape(x.shape[0], x.shape[1], per_chan * piece)

    raw6 = jnp.concatenate(
        [shift_rows(image[-1:], upward=False), image, shift_rows(image[:1], upward=True)], axis=0
    )
    send_rows = lax.dynamic_slice_in_dim(raw6, 2 * lo, height, axis=0)
    sent_img = lax.ppermute(local_subset(send_rows, 1 - lo), "lo", [(0, 1), (1, 0)])
    own_img = local_subset(raw6, lo)
    block_piece = lax.dynamic_slice_in_dim(
        jnp.concatenate([sent_img, own_img, sent_img], axis=0), height * (1 - lo), 2 * height + 2, axis=0
    )
    img_block = lax.all_gather(block_piece, "chan", axis=2, tiled=True)

    interior = taps(gathered, 1)
    interior = interior + jnp.pad(taps(gathered[:-1], 0), ((1, 0), (0, 0), (0, 0), (0, 0)))
    interior = interior + jnp.pad(taps(gathered[1:], 2), ((0, 1), (0, 0), (0, 0), (0, 0)))
    conv_sum = shift_sum(interior)
    conv_sum = conv_sum + jnp.concatenate(
        [to_next, jnp.zeros((height - 2, breadth, local_filters), jnp.float32), to_prev], axis=0
    )
    conv_out = conv_sum.astype(jnp.bfloat16)

    conv_wide = conv_out.astype(jnp.float32)
    upstream = grad_filters.astype(jnp.float32)
    partial = jnp.stack(
        [jnp.sum(conv_wide * conv_wide, axis=-1), jnp.sum(upstream * conv_wide, axis=-1)], axis=-1
    )
    totals = lax.psum(partial, "chan")
    inverse_rms = lax.rsqrt(totals[..., 0:1] / all_filters + 1e-06)
    mean_gu = inverse_rms * (totals[..., 1:2] / all_filters)
    unit = conv_wide * inverse_rms
    normed_filters = unit.astype(jnp.bfloat16)
    grad_conv = (inverse_rms * (upstream - unit * mean_gu)).astype(jnp.bfloat16)

    sent_grad = lax.ppermute(grad_conv, "lo", [(0, 1), (1, 0)])
    img_block = jnp.pad(img_block, ((0, 0), (1, 1), (0, 0)))
    width_w = img_block.shape[2]

    def pair_part(grad_rows, first_row):
        flat = grad_rows.reshape(height * breadth, local_filters)
        blocks = []
        for weight_tap_row in range(3):
            rows = lax.dynamic_slice_in_dim(img_block, first_row + weight_tap_row, height, axis=0)
            for weight_tap_col in range(3):
                weight_window = rows[:, weight_tap_col : weight_tap_col + breadth].reshape(height * breadth, width_w)
                blocks.append(
                    lax.dot_general(
                        weight_window,
                        flat,
                        (((0,), (0,)), ((), ())),
                        preferred_element_type=jnp.float32,
                    )
                )
        return jnp.stack(blocks)

    own_part = pair_part(grad_conv, height * lo)
    sent_grad, own_part = lax.optimization_barrier((sent_grad, own_part))
    stacked = (own_part + pair_part(sent_grad, height * (1 - lo))).reshape(3, 3, width_w, local_filters)
    normed_late, _ = lax.optimization_barrier((normed_filters, stacked))
    normed = lax.all_to_all(normed_late, "chan", split_axis=1, concat_axis=2, tiled=True)
    grad_weight = lax.psum_scatter(
        stacked.astype(jnp.bfloat16), "hi", scatter_dimension=2, tiled=True
    ).astype(jnp.float32)

    grad_rimmed = jnp.concatenate(
        [shift_rows(grad_conv[-1:], upward=False), grad_conv, shift_rows(grad_conv[:1], upward=True)], axis=0
    )
    grad_padded = jnp.pad(grad_rimmed, ((0, 0), (1, 1), (0, 0)))
    columns = jnp.concatenate(
        [
            grad_padded[2 - a : 2 - a + height, 2 - b : 2 - b + breadth]
            for a in range(3)
            for b in range(3)
        ],
        axis=-1,
    ).reshape(height * breadth, 9 * local_filters)
    by_filter = jnp.transpose(weight, (0, 1, 3, 2)).reshape(9 * local_filters, all_chans)
    group = all_chans // chans
    split = jnp.stack(
        [
            jnp.dot(columns, by_filter[:, j * group : (j + 1) * group], preferred_element_type=jnp.float32)
            for j in range(chans)
        ]
    ).astype(jnp.bfloat16)
    received = lax.all_to_all(split, "chan", split_axis=0, concat_axis=0, tiled=True)
    grad_input = jnp.sum(received.astype(jnp.float32), axis=0).astype(jnp.bfloat16).reshape(height, breadth, group)
    return (normed, grad_input, grad_weight)


def solution(mesh):
    slabs = mesh.shape["slab"]
    chans = mesh.shape["chan"]
    split_mesh = Mesh(mesh.devices.reshape(slabs // 2, 2, chans), ("hi", "lo", "chan"))
    return jax.shard_map(
        on_device,
        mesh=split_mesh,
        in_specs=(P(SLAB, None, "chan"), P(None, None, None, "chan"), P(SLAB, "chan", None)),
        out_specs=(P(SLAB, "chan", None), P(SLAB, None, "chan"), P(None, None, SLAB, "chan")),
        check_vma=False,
    )
```

```python
import jax
import jax.numpy as jnp
from jax import lax
from jax.sharding import Mesh
from jax.sharding import PartitionSpec as P

SLAB = ("hi", "lo")


def shift_rows(rows, upward):
    count = lax.axis_size(SLAB)
    if upward:
        pairs = [((i + 1), i) for i in range(count - 1)]
    else:
        pairs = [(i, i + 1) for i in range(count - 1)]
    return lax.ppermute(rows, SLAB, pairs)


def shift_sum(z):
    breadth = z.shape[-3]
    widths = [(0, 0)] * (z.ndim - 3) + [(1, 1), (0, 0), (0, 0)]
    zp = jnp.pad(z, widths)
    return zp[..., 0:breadth, 0, :] + zp[..., 1 : breadth + 1, 1, :] + zp[..., 2 : breadth + 2, 2, :]


def on_device(image, weight, grad_out):
    height = image.shape[0]
    breadth = image.shape[1]
    local_chans = image.shape[2]
    all_chans = weight.shape[2]
    local_filters = weight.shape[3]
    chans = lax.axis_size("chan")
    all_filters = local_filters * chans
    n_hi = lax.axis_size("hi")
    n_lo = lax.axis_size("lo")
    lo = lax.axis_index("lo")
    piece = all_chans // (n_hi * n_lo)
    per_chan = local_chans // (n_lo * piece)

    grad_filters = lax.all_to_all(grad_out, "chan", split_axis=2, concat_axis=1, tiled=True)
    gathered = lax.all_gather(image, "chan", axis=2, tiled=True)

    by_row = jnp.transpose(weight, (0, 2, 1, 3)).reshape(3, all_chans, 3 * local_filters)

    def taps(rows, a):
        count = rows.shape[0]
        flat = rows.reshape(count * breadth, all_chans)
        out = jnp.dot(flat, by_row[a], preferred_element_type=jnp.float32)
        return out.reshape(count, breadth, 3, local_filters)

    to_next = lax.ppermute(shift_sum(taps(gathered[-1:], 0)), SLAB, [(i, i + 1) for i in range(lax.axis_size(SLAB) - 1)])
    to_prev = lax.ppermute(shift_sum(taps(gathered[:1], 2)), SLAB, [(i + 1, i) for i in range(lax.axis_size(SLAB) - 1)])

    def local_subset(x, which):
        shaped = x.reshape(x.shape[0], x.shape[1], per_chan, n_lo, piece)
        taken = lax.dynamic_index_in_dim(shaped, which, axis=3, keepdims=False)
        return taken.reshape(x.shape[0], x.shape[1], per_chan * piece)

    raw6 = jnp.concatenate(
        [shift_rows(image[-1:], upward=False), image, shift_rows(image[:1], upward=True)], axis=0
    )
    send_rows = lax.dynamic_slice_in_dim(raw6, 2 * lo, height, axis=0)
    sent_img = lax.ppermute(local_subset(send_rows, 1 - lo), "lo", [(0, 1), (1, 0)])
    own_img = local_subset(raw6, lo)
    block_piece = lax.dynamic_slice_in_dim(
        jnp.concatenate([sent_img, own_img, sent_img], axis=0), height * (1 - lo), 2 * height + 2, axis=0
    )
    img_block = lax.all_gather(block_piece, "chan", axis=2, tiled=True)

    interior = taps(gathered, 1)
    interior = interior + jnp.pad(taps(gathered[:-1], 0), ((1, 0), (0, 0), (0, 0), (0, 0)))
    interior = interior + jnp.pad(taps(gathered[1:], 2), ((0, 1), (0, 0), (0, 0), (0, 0)))
    conv_sum = shift_sum(interior)
    conv_sum = conv_sum + jnp.concatenate(
        [to_next, jnp.zeros((height - 2, breadth, local_filters), jnp.float32), to_prev], axis=0
    )
    conv_out = conv_sum.astype(jnp.bfloat16)

    conv_wide = conv_out.astype(jnp.float32)
    upstream = grad_filters.astype(jnp.float32)
    partial = jnp.stack(
        [jnp.sum(conv_wide * conv_wide, axis=-1), jnp.sum(upstream * conv_wide, axis=-1)], axis=-1
    )
    totals = lax.psum(partial, "chan")
    inverse_rms = lax.rsqrt(totals[..., 0:1] / all_filters + 1e-06)
    mean_gu = inverse_rms * (totals[..., 1:2] / all_filters)
    unit = conv_wide * inverse_rms
    normed_filters = unit.astype(jnp.bfloat16)
    grad_conv = (inverse_rms * (upstream - unit * mean_gu)).astype(jnp.bfloat16)
    normed = lax.all_to_all(normed_filters, "chan", split_axis=1, concat_axis=2, tiled=True)

    sent_grad = lax.ppermute(grad_conv, "lo", [(0, 1), (1, 0)])
    img_block = jnp.pad(img_block, ((0, 0), (1, 1), (0, 0)))
    width_w = img_block.shape[2]

    def pair_part(grad_rows, first_row):
        flat = grad_rows.reshape(height * breadth, local_filters)
        blocks = []
        for weight_tap_row in range(3):
            rows = lax.dynamic_slice_in_dim(img_block, first_row + weight_tap_row, height, axis=0)
            for weight_tap_col in range(3):
                weight_window = rows[:, weight_tap_col : weight_tap_col + breadth].reshape(height * breadth, width_w)
                blocks.append(
                    lax.dot_general(
                        weight_window,
                        flat,
                        (((0,), (0,)), ((), ())),
                        preferred_element_type=jnp.float32,
                    )
                )
        return jnp.stack(blocks)

    own_part = pair_part(grad_conv, height * lo)
    sent_grad, own_part = lax.optimization_barrier((sent_grad, own_part))
    stacked = (own_part + pair_part(sent_grad, height * (1 - lo))).reshape(3, 3, width_w, local_filters)
    grad_weight = lax.psum_scatter(
        stacked.astype(jnp.bfloat16), "hi", scatter_dimension=2, tiled=True
    ).astype(jnp.float32)

    count = lax.axis_size(SLAB)
    crossing = [(s, s + 1) for s in range(1, count - 1, 2)] + [(s, s - 1) for s in range(2, count, 2)]
    cross = lax.ppermute(jnp.where(lo == 1, grad_conv[-1:], grad_conv[:1]), SLAB, crossing)
    top = jnp.where(lo == 0, cross, sent_grad[-1:])
    bottom = jnp.where(lo == 0, sent_grad[:1], cross)
    grad_rimmed = jnp.concatenate([top, grad_conv, bottom], axis=0)
    grad_padded = jnp.pad(grad_rimmed, ((0, 0), (1, 1), (0, 0)))
    columns = jnp.concatenate(
        [
            grad_padded[2 - a : 2 - a + height, 2 - b : 2 - b + breadth]
            for a in range(3)
            for b in range(3)
        ],
        axis=-1,
    ).reshape(height * breadth, 9 * local_filters)
    by_filter = jnp.transpose(weight, (0, 1, 3, 2)).reshape(9 * local_filters, all_chans)
    input_term = lax.dot_general(
        by_filter, columns, (((0,), (1,)), ((), ())), preferred_element_type=jnp.float32
    )
    group = all_chans // chans
    split = input_term.astype(jnp.bfloat16).reshape(chans, group, height * breadth)
    received = lax.all_to_all(split, "chan", split_axis=0, concat_axis=0, tiled=True)
    summed = jnp.sum(received.astype(jnp.float32), axis=0)
    grad_input = jnp.transpose(summed).astype(jnp.bfloat16).reshape(height, breadth, group)
    return (normed, grad_input, grad_weight)


def solution(mesh):
    slabs = mesh.shape["slab"]
    chans = mesh.shape["chan"]
    split_mesh = Mesh(mesh.devices.reshape(slabs // 2, 2, chans), ("hi", "lo", "chan"))
    return jax.shard_map(
        on_device,
        mesh=split_mesh,
        in_specs=(P(SLAB, None, "chan"), P(None, None, None, "chan"), P(SLAB, "chan", None)),
        out_specs=(P(SLAB, "chan", None), P(SLAB, None, "chan"), P(None, None, SLAB, "chan")),
        check_vma=False,
    )
```

```python
import jax
import jax.numpy as jnp
from jax import lax
from jax.sharding import Mesh
from jax.sharding import PartitionSpec as P

SLAB = ("hi", "lo")


def shift_rows(rows, upward):
    count = lax.axis_size(SLAB)
    if upward:
        pairs = [((i + 1), i) for i in range(count - 1)]
    else:
        pairs = [(i, i + 1) for i in range(count - 1)]
    return lax.ppermute(rows, SLAB, pairs)


def shift_sum(z):
    breadth = z.shape[-3]
    widths = [(0, 0)] * (z.ndim - 3) + [(1, 1), (0, 0), (0, 0)]
    zp = jnp.pad(z, widths)
    return zp[..., 0:breadth, 0, :] + zp[..., 1 : breadth + 1, 1, :] + zp[..., 2 : breadth + 2, 2, :]


def on_device(image, weight, grad_out):
    height = image.shape[0]
    breadth = image.shape[1]
    local_chans = image.shape[2]
    all_chans = weight.shape[2]
    local_filters = weight.shape[3]
    chans = lax.axis_size("chan")
    all_filters = local_filters * chans
    n_hi = lax.axis_size("hi")
    n_lo = lax.axis_size("lo")
    lo = lax.axis_index("lo")
    piece = all_chans // (n_hi * n_lo)
    per_chan = local_chans // (n_lo * piece)

    grad_filters = lax.all_to_all(grad_out, "chan", split_axis=2, concat_axis=1, tiled=True)
    gathered = lax.all_gather(image, "chan", axis=2, tiled=True)

    def taps(rows, a):
        count = rows.shape[0]
        flat = rows.reshape(count * breadth, all_chans)
        out = jnp.stack(
            [jnp.dot(flat, weight[a, b], preferred_element_type=jnp.float32) for b in range(3)], axis=1
        )
        return out.reshape(count, breadth, 3, local_filters)

    to_next = lax.ppermute(shift_sum(taps(gathered[-1:], 0)), SLAB, [(i, i + 1) for i in range(lax.axis_size(SLAB) - 1)])
    to_prev = lax.ppermute(shift_sum(taps(gathered[:1], 2)), SLAB, [(i + 1, i) for i in range(lax.axis_size(SLAB) - 1)])

    def local_subset(x, which):
        shaped = x.reshape(x.shape[0], x.shape[1], per_chan, n_lo, piece)
        taken = lax.dynamic_index_in_dim(shaped, which, axis=3, keepdims=False)
        return taken.reshape(x.shape[0], x.shape[1], per_chan * piece)

    raw6 = jnp.concatenate(
        [shift_rows(image[-1:], upward=False), image, shift_rows(image[:1], upward=True)], axis=0
    )
    send_rows = lax.dynamic_slice_in_dim(raw6, 2 * lo, height, axis=0)
    sent_img = lax.ppermute(local_subset(send_rows, 1 - lo), "lo", [(0, 1), (1, 0)])
    own_img = local_subset(raw6, lo)
    block_piece = lax.dynamic_slice_in_dim(
        jnp.concatenate([sent_img, own_img, sent_img], axis=0), height * (1 - lo), 2 * height + 2, axis=0
    )
    img_block = lax.all_gather(block_piece, "chan", axis=2, tiled=True)

    interior = taps(gathered, 1)
    interior = interior + jnp.pad(taps(gathered[:-1], 0), ((1, 0), (0, 0), (0, 0), (0, 0)))
    interior = interior + jnp.pad(taps(gathered[1:], 2), ((0, 1), (0, 0), (0, 0), (0, 0)))
    conv_sum = shift_sum(interior)
    conv_sum = conv_sum + jnp.concatenate(
        [to_next, jnp.zeros((height - 2, breadth, local_filters), jnp.float32), to_prev], axis=0
    )
    conv_out = conv_sum.astype(jnp.bfloat16)

    conv_wide = conv_out.astype(jnp.float32)
    upstream = grad_filters.astype(jnp.float32)
    partial = jnp.stack(
        [jnp.sum(conv_wide * conv_wide, axis=-1), jnp.sum(upstream * conv_wide, axis=-1)], axis=-1
    )
    totals = lax.psum(partial, "chan")
    inverse_rms = lax.rsqrt(totals[..., 0:1] / all_filters + 1e-06)
    mean_gu = inverse_rms * (totals[..., 1:2] / all_filters)
    unit = conv_wide * inverse_rms
    normed_filters = unit.astype(jnp.bfloat16)
    grad_conv = (inverse_rms * (upstream - unit * mean_gu)).astype(jnp.bfloat16)
    normed = lax.all_to_all(normed_filters, "chan", split_axis=1, concat_axis=2, tiled=True)

    sent_grad = lax.ppermute(grad_conv, "lo", [(0, 1), (1, 0)])
    img_block = jnp.pad(img_block, ((0, 0), (1, 1), (0, 0)))
    width_w = img_block.shape[2]

    def pair_part(grad_rows, first_row):
        flat = grad_rows.reshape(height * breadth, local_filters)
        blocks = []
        for weight_tap_row in range(3):
            rows = lax.dynamic_slice_in_dim(img_block, first_row + weight_tap_row, height, axis=0)
            for weight_tap_col in range(3):
                weight_window = rows[:, weight_tap_col : weight_tap_col + breadth].reshape(height * breadth, width_w)
                blocks.append(
                    lax.dot_general(
                        weight_window,
                        flat,
                        (((0,), (0,)), ((), ())),
                        preferred_element_type=jnp.float32,
                    )
                )
        return jnp.stack(blocks)

    own_part = pair_part(grad_conv, height * lo)
    sent_grad, own_part = lax.optimization_barrier((sent_grad, own_part))
    stacked = (own_part + pair_part(sent_grad, height * (1 - lo))).reshape(3, 3, width_w, local_filters)
    grad_weight = lax.psum_scatter(
        stacked.astype(jnp.bfloat16), "hi", scatter_dimension=2, tiled=True
    ).astype(jnp.float32)

    count = lax.axis_size(SLAB)
    crossing = [(s, s + 1) for s in range(1, count - 1, 2)] + [(s, s - 1) for s in range(2, count, 2)]
    cross = lax.ppermute(jnp.where(lo == 1, grad_conv[-1:], grad_conv[:1]), SLAB, crossing)
    top = jnp.where(lo == 0, cross, sent_grad[-1:])
    bottom = jnp.where(lo == 0, sent_grad[:1], cross)
    grad_rimmed = jnp.concatenate([top, grad_conv, bottom], axis=0)
    grad_padded = jnp.pad(grad_rimmed, ((0, 0), (1, 1), (0, 0)))
    columns = jnp.concatenate(
        [
            grad_padded[2 - a : 2 - a + height, 2 - b : 2 - b + breadth]
            for a in range(3)
            for b in range(3)
        ],
        axis=-1,
    ).reshape(height * breadth, 9 * local_filters)
    weight_late, _ = lax.optimization_barrier((weight, stacked))
    by_filter = jnp.transpose(weight_late, (0, 1, 3, 2)).reshape(9 * local_filters, all_chans)
    input_term = lax.dot_general(
        by_filter, columns, (((0,), (1,)), ((), ())), preferred_element_type=jnp.float32
    )
    group = all_chans // chans
    split = input_term.astype(jnp.bfloat16).reshape(chans, group, height * breadth)
    received = lax.all_to_all(split, "chan", split_axis=0, concat_axis=0, tiled=True)
    summed = jnp.sum(received.astype(jnp.float32), axis=0)
    grad_input = jnp.transpose(summed).astype(jnp.bfloat16).reshape(height, breadth, group)
    return (normed, grad_input, grad_weight)


def solution(mesh):
    slabs = mesh.shape["slab"]
    chans = mesh.shape["chan"]
    split_mesh = Mesh(mesh.devices.reshape(slabs // 2, 2, chans), ("hi", "lo", "chan"))
    return jax.shard_map(
        on_device,
        mesh=split_mesh,
        in_specs=(P(SLAB, None, "chan"), P(None, None, None, "chan"), P(SLAB, "chan", None)),
        out_specs=(P(SLAB, "chan", None), P(SLAB, None, "chan"), P(None, None, SLAB, "chan")),
        check_vma=False,
    )
```

```python
import jax
import jax.numpy as jnp
from jax import lax
from jax.sharding import Mesh
from jax.sharding import PartitionSpec as P

SLAB = ("hi", "lo")


def shift_rows(rows, upward):
    count = lax.axis_size(SLAB)
    if upward:
        pairs = [((i + 1), i) for i in range(count - 1)]
    else:
        pairs = [(i, i + 1) for i in range(count - 1)]
    return lax.ppermute(rows, SLAB, pairs)


def shift_sum(z):
    breadth = z.shape[-3]
    widths = [(0, 0)] * (z.ndim - 3) + [(1, 1), (0, 0), (0, 0)]
    zp = jnp.pad(z, widths)
    return zp[..., 0:breadth, 0, :] + zp[..., 1 : breadth + 1, 1, :] + zp[..., 2 : breadth + 2, 2, :]


def on_device(image, weight, grad_out):
    height = image.shape[0]
    breadth = image.shape[1]
    local_chans = image.shape[2]
    all_chans = weight.shape[2]
    local_filters = weight.shape[3]
    chans = lax.axis_size("chan")
    all_filters = local_filters * chans
    n_hi = lax.axis_size("hi")
    n_lo = lax.axis_size("lo")
    lo = lax.axis_index("lo")
    piece = all_chans // (n_hi * n_lo)
    per_chan = local_chans // (n_lo * piece)

    grad_filters = lax.all_to_all(grad_out, "chan", split_axis=2, concat_axis=1, tiled=True)
    gathered = lax.all_gather(image, "chan", axis=2, tiled=True)

    by_row = jnp.transpose(weight, (0, 2, 1, 3)).reshape(3, all_chans, 3 * local_filters)

    def taps(rows, a):
        count = rows.shape[0]
        flat = rows.reshape(count * breadth, all_chans)
        out = jnp.dot(flat, by_row[a], preferred_element_type=jnp.float32)
        return out.reshape(count, breadth, 3, local_filters)

    to_next = lax.ppermute(shift_sum(taps(gathered[-1:], 0)), SLAB, [(i, i + 1) for i in range(lax.axis_size(SLAB) - 1)])
    to_prev = lax.ppermute(shift_sum(taps(gathered[:1], 2)), SLAB, [(i + 1, i) for i in range(lax.axis_size(SLAB) - 1)])

    def local_subset(x, which):
        shaped = x.reshape(x.shape[0], x.shape[1], per_chan, n_lo, piece)
        taken = lax.dynamic_index_in_dim(shaped, which, axis=3, keepdims=False)
        return taken.reshape(x.shape[0], x.shape[1], per_chan * piece)

    count = lax.axis_size(SLAB)
    crossing = [(s, s + 1) for s in range(1, count - 1, 2)] + [(s, s - 1) for s in range(2, count, 2)]
    edge = lax.ppermute(jnp.where(lo == 1, image[-1:], image[:1]), SLAB, crossing)
    mine = jnp.where(
        lo == 0, jnp.concatenate([edge, image], axis=0), jnp.concatenate([image, edge], axis=0)
    )
    sent_img = lax.ppermute(local_subset(mine, 1 - lo), "lo", [(0, 1), (1, 0)])
    own_img = local_subset(mine, lo)
    block_piece = lax.dynamic_slice_in_dim(
        jnp.concatenate([sent_img, own_img, sent_img], axis=0), (height + 1) * (1 - lo), 2 * height + 2, axis=0
    )
    img_block = lax.all_gather(block_piece, "chan", axis=2, tiled=True)

    interior = taps(gathered, 1)
    interior = interior + jnp.pad(taps(gathered[:-1], 0), ((1, 0), (0, 0), (0, 0), (0, 0)))
    interior = interior + jnp.pad(taps(gathered[1:], 2), ((0, 1), (0, 0), (0, 0), (0, 0)))
    conv_sum = shift_sum(interior)
    conv_sum = conv_sum + jnp.concatenate(
        [to_next, jnp.zeros((height - 2, breadth, local_filters), jnp.float32), to_prev], axis=0
    )
    conv_out = conv_sum.astype(jnp.bfloat16)

    conv_wide = conv_out.astype(jnp.float32)
    upstream = grad_filters.astype(jnp.float32)
    partial = jnp.stack(
        [jnp.sum(conv_wide * conv_wide, axis=-1), jnp.sum(upstream * conv_wide, axis=-1)], axis=-1
    )
    totals = lax.psum(partial, "chan")
    inverse_rms = lax.rsqrt(totals[..., 0:1] / all_filters + 1e-06)
    mean_gu = inverse_rms * (totals[..., 1:2] / all_filters)
    unit = conv_wide * inverse_rms
    normed_filters = unit.astype(jnp.bfloat16)
    grad_conv = (inverse_rms * (upstream - unit * mean_gu)).astype(jnp.bfloat16)
    normed = lax.all_to_all(normed_filters, "chan", split_axis=1, concat_axis=2, tiled=True)

    sent_grad = lax.ppermute(grad_conv, "lo", [(0, 1), (1, 0)])
    img_block = jnp.pad(img_block, ((0, 0), (1, 1), (0, 0)))
    width_w = img_block.shape[2]

    def pair_part(grad_rows, first_row):
        flat = grad_rows.reshape(height * breadth, local_filters)
        blocks = []
        for weight_tap_row in range(3):
            rows = lax.dynamic_slice_in_dim(img_block, first_row + weight_tap_row, height, axis=0)
            for weight_tap_col in range(3):
                weight_window = rows[:, weight_tap_col : weight_tap_col + breadth].reshape(height * breadth, width_w)
                blocks.append(
                    lax.dot_general(
                        weight_window,
                        flat,
                        (((0,), (0,)), ((), ())),
                        preferred_element_type=jnp.float32,
                    )
                )
        return jnp.stack(blocks)

    own_part = pair_part(grad_conv, height * lo)
    sent_grad, own_part = lax.optimization_barrier((sent_grad, own_part))
    stacked = (own_part + pair_part(sent_grad, height * (1 - lo))).reshape(3, 3, width_w, local_filters)
    grad_weight = lax.psum_scatter(
        stacked.astype(jnp.bfloat16), "hi", scatter_dimension=2, tiled=True
    ).astype(jnp.float32)

    count = lax.axis_size(SLAB)
    crossing = [(s, s + 1) for s in range(1, count - 1, 2)] + [(s, s - 1) for s in range(2, count, 2)]
    cross = lax.ppermute(jnp.where(lo == 1, grad_conv[-1:], grad_conv[:1]), SLAB, crossing)
    top = jnp.where(lo == 0, cross, sent_grad[-1:])
    bottom = jnp.where(lo == 0, sent_grad[:1], cross)
    grad_rimmed = jnp.concatenate([top, grad_conv, bottom], axis=0)
    grad_padded = jnp.pad(grad_rimmed, ((0, 0), (1, 1), (0, 0)))
    columns = jnp.concatenate(
        [
            grad_padded[2 - a : 2 - a + height, 2 - b : 2 - b + breadth]
            for a in range(3)
            for b in range(3)
        ],
        axis=-1,
    ).reshape(height * breadth, 9 * local_filters)
    by_filter = jnp.transpose(weight, (0, 1, 3, 2)).reshape(9 * local_filters, all_chans)
    input_term = lax.dot_general(
        by_filter, columns, (((0,), (1,)), ((), ())), preferred_element_type=jnp.float32
    )
    group = all_chans // chans
    split = input_term.astype(jnp.bfloat16).reshape(chans, group, height * breadth)
    received = lax.all_to_all(split, "chan", split_axis=0, concat_axis=0, tiled=True)
    summed = jnp.sum(received.astype(jnp.float32), axis=0)
    grad_input = jnp.transpose(summed).astype(jnp.bfloat16).reshape(height, breadth, group)
    return (normed, grad_input, grad_weight)


def solution(mesh):
    slabs = mesh.shape["slab"]
    chans = mesh.shape["chan"]
    split_mesh = Mesh(mesh.devices.reshape(slabs // 2, 2, chans), ("hi", "lo", "chan"))
    return jax.shard_map(
        on_device,
        mesh=split_mesh,
        in_specs=(P(SLAB, None, "chan"), P(None, None, None, "chan"), P(SLAB, "chan", None)),
        out_specs=(P(SLAB, "chan", None), P(SLAB, None, "chan"), P(None, None, SLAB, "chan")),
        check_vma=False,
    )
```

```python
import jax
import jax.numpy as jnp
from jax import lax
from jax.sharding import Mesh
from jax.sharding import PartitionSpec as P

SLAB = ("hi", "lo")


def shift_rows(rows, upward):
    count = lax.axis_size(SLAB)
    if upward:
        pairs = [((i + 1), i) for i in range(count - 1)]
    else:
        pairs = [(i, i + 1) for i in range(count - 1)]
    return lax.ppermute(rows, SLAB, pairs)


def shift_sum(z):
    breadth = z.shape[-3]
    widths = [(0, 0)] * (z.ndim - 3) + [(1, 1), (0, 0), (0, 0)]
    zp = jnp.pad(z, widths)
    return zp[..., 0:breadth, 0, :] + zp[..., 1 : breadth + 1, 1, :] + zp[..., 2 : breadth + 2, 2, :]


def on_device(image, weight, grad_out):
    height = image.shape[0]
    breadth = image.shape[1]
    local_chans = image.shape[2]
    all_chans = weight.shape[2]
    local_filters = weight.shape[3]
    chans = lax.axis_size("chan")
    all_filters = local_filters * chans
    n_hi = lax.axis_size("hi")
    n_lo = lax.axis_size("lo")
    lo = lax.axis_index("lo")
    piece = all_chans // (n_hi * n_lo)
    per_chan = local_chans // (n_lo * piece)

    grad_filters = lax.all_to_all(grad_out, "chan", split_axis=2, concat_axis=1, tiled=True)
    gathered = lax.all_gather(image, "chan", axis=2, tiled=True)

    by_row = jnp.transpose(weight, (0, 2, 1, 3)).reshape(3, all_chans, 3 * local_filters)

    def taps(rows, a):
        count = rows.shape[0]
        flat = rows.reshape(count * breadth, all_chans)
        out = jnp.dot(flat, by_row[a], preferred_element_type=jnp.float32)
        return out.reshape(count, breadth, 3, local_filters)

    to_next = lax.ppermute(shift_sum(taps(gathered[-1:], 0)), SLAB, [(i, i + 1) for i in range(lax.axis_size(SLAB) - 1)])
    to_prev = lax.ppermute(shift_sum(taps(gathered[:1], 2)), SLAB, [(i + 1, i) for i in range(lax.axis_size(SLAB) - 1)])

    def local_subset(x, which):
        shaped = x.reshape(x.shape[0], x.shape[1], per_chan, n_lo, piece)
        taken = lax.dynamic_index_in_dim(shaped, which, axis=3, keepdims=False)
        return taken.reshape(x.shape[0], x.shape[1], per_chan * piece)

    raw6 = jnp.concatenate(
        [shift_rows(image[-1:], upward=False), image, shift_rows(image[:1], upward=True)], axis=0
    )
    send_rows = lax.dynamic_slice_in_dim(raw6, 2 * lo, height, axis=0)
    sent_img = lax.ppermute(local_subset(send_rows, 1 - lo), "lo", [(0, 1), (1, 0)])
    own_img = local_subset(raw6, lo)
    block_piece = lax.dynamic_slice_in_dim(
        jnp.concatenate([sent_img, own_img, sent_img], axis=0), height * (1 - lo), 2 * height + 2, axis=0
    )
    img_block = lax.all_gather(block_piece, "chan", axis=2, tiled=True)

    interior = taps(gathered, 1)
    interior = interior + jnp.pad(taps(gathered[:-1], 0), ((1, 0), (0, 0), (0, 0), (0, 0)))
    interior = interior + jnp.pad(taps(gathered[1:], 2), ((0, 1), (0, 0), (0, 0), (0, 0)))
    conv_sum = shift_sum(interior)
    conv_sum = conv_sum + jnp.concatenate(
        [to_next, jnp.zeros((height - 2, breadth, local_filters), jnp.float32), to_prev], axis=0
    )
    conv_out = conv_sum.astype(jnp.bfloat16)

    conv_wide = conv_out.astype(jnp.float32)
    upstream = grad_filters.astype(jnp.float32)
    partial = jnp.stack(
        [jnp.sum(conv_wide * conv_wide, axis=-1), jnp.sum(upstream * conv_wide, axis=-1)], axis=-1
    )
    totals = lax.psum(partial, "chan")
    inverse_rms = lax.rsqrt(totals[..., 0:1] / all_filters + 1e-06)
    mean_gu = inverse_rms * (totals[..., 1:2] / all_filters)
    unit = conv_wide * inverse_rms
    normed_filters = unit.astype(jnp.bfloat16)
    grad_conv = (inverse_rms * (upstream - unit * mean_gu)).astype(jnp.bfloat16)

    sent_grad = lax.ppermute(grad_conv, "lo", [(0, 1), (1, 0)])
    img_block = jnp.pad(img_block, ((0, 0), (1, 1), (0, 0)))
    width_w = img_block.shape[2]

    def pair_part(grad_rows, first_row):
        flat = grad_rows.reshape(height * breadth, local_filters)
        blocks = []
        for weight_tap_row in range(3):
            rows = lax.dynamic_slice_in_dim(img_block, first_row + weight_tap_row, height, axis=0)
            for weight_tap_col in range(3):
                weight_window = rows[:, weight_tap_col : weight_tap_col + breadth].reshape(height * breadth, width_w)
                blocks.append(
                    lax.dot_general(
                        weight_window,
                        flat,
                        (((0,), (0,)), ((), ())),
                        preferred_element_type=jnp.float32,
                    )
                )
        return jnp.stack(blocks)

    own_part = pair_part(grad_conv, height * lo)
    sent_grad, own_part = lax.optimization_barrier((sent_grad, own_part))
    stacked = (own_part + pair_part(sent_grad, height * (1 - lo))).reshape(3, 3, width_w, local_filters)
    grad_weight = lax.psum_scatter(
        stacked.astype(jnp.bfloat16), "hi", scatter_dimension=2, tiled=True
    ).astype(jnp.float32)

    count = lax.axis_size(SLAB)
    crossing = [(s, s + 1) for s in range(1, count - 1, 2)] + [(s, s - 1) for s in range(2, count, 2)]
    cross = lax.ppermute(jnp.where(lo == 1, grad_conv[-1:], grad_conv[:1]), SLAB, crossing)
    top = jnp.where(lo == 0, cross, sent_grad[-1:])
    bottom = jnp.where(lo == 0, sent_grad[:1], cross)
    grad_rimmed = jnp.concatenate([top, grad_conv, bottom], axis=0)
    grad_padded = jnp.pad(grad_rimmed, ((0, 0), (1, 1), (0, 0)))
    columns = jnp.concatenate(
        [
            grad_padded[2 - a : 2 - a + height, 2 - b : 2 - b + breadth]
            for a in range(3)
            for b in range(3)
        ],
        axis=-1,
    ).reshape(height * breadth, 9 * local_filters)
    by_filter = jnp.transpose(weight, (0, 1, 3, 2)).reshape(9 * local_filters, all_chans)
    input_term = lax.dot_general(
        by_filter, columns, (((0,), (1,)), ((), ())), preferred_element_type=jnp.float32
    )
    group = all_chans // chans
    split = input_term.astype(jnp.bfloat16).reshape(chans, group, height * breadth)
    received = lax.all_to_all(split, "chan", split_axis=0, concat_axis=0, tiled=True)
    normed_late, _ = lax.optimization_barrier((normed_filters, split))
    normed = lax.all_to_all(normed_late, "chan", split_axis=1, concat_axis=2, tiled=True)
    summed = jnp.sum(received.astype(jnp.float32), axis=0)
    grad_input = jnp.transpose(summed).astype(jnp.bfloat16).reshape(height, breadth, group)
    return (normed, grad_input, grad_weight)


def solution(mesh):
    slabs = mesh.shape["slab"]
    chans = mesh.shape["chan"]
    split_mesh = Mesh(mesh.devices.reshape(slabs // 2, 2, chans), ("hi", "lo", "chan"))
    return jax.shard_map(
        on_device,
        mesh=split_mesh,
        in_specs=(P(SLAB, None, "chan"), P(None, None, None, "chan"), P(SLAB, "chan", None)),
        out_specs=(P(SLAB, "chan", None), P(SLAB, None, "chan"), P(None, None, SLAB, "chan")),
        check_vma=False,
    )
```

```python
import jax
import jax.numpy as jnp
from jax import lax
from jax.sharding import Mesh
from jax.sharding import PartitionSpec as P

SLAB = ("hi", "lo")


def shift_rows(rows, upward):
    count = lax.axis_size(SLAB)
    if upward:
        pairs = [((i + 1), i) for i in range(count - 1)]
    else:
        pairs = [(i, i + 1) for i in range(count - 1)]
    return lax.ppermute(rows, SLAB, pairs)


def shift_sum(z):
    breadth = z.shape[-3]
    widths = [(0, 0)] * (z.ndim - 3) + [(1, 1), (0, 0), (0, 0)]
    zp = jnp.pad(z, widths)
    return zp[..., 0:breadth, 0, :] + zp[..., 1 : breadth + 1, 1, :] + zp[..., 2 : breadth + 2, 2, :]


def on_device(image, weight, grad_out):
    height = image.shape[0]
    breadth = image.shape[1]
    local_chans = image.shape[2]
    all_chans = weight.shape[2]
    local_filters = weight.shape[3]
    chans = lax.axis_size("chan")
    all_filters = local_filters * chans
    n_hi = lax.axis_size("hi")
    n_lo = lax.axis_size("lo")
    lo = lax.axis_index("lo")
    piece = all_chans // (n_hi * n_lo)
    per_chan = local_chans // (n_lo * piece)

    grad_filters = lax.all_to_all(grad_out, "chan", split_axis=2, concat_axis=1, tiled=True)
    gathered = lax.all_gather(image, "chan", axis=2, tiled=True)

    def taps(rows, a):
        count = rows.shape[0]
        flat = rows.reshape(count * breadth, all_chans)
        out = lax.dot_general(flat, weight[a], (((1,), (1,)), ((), ())), preferred_element_type=jnp.float32)
        return out.reshape(count, breadth, 3, local_filters)

    to_next = lax.ppermute(shift_sum(taps(gathered[-1:], 0)), SLAB, [(i, i + 1) for i in range(lax.axis_size(SLAB) - 1)])
    to_prev = lax.ppermute(shift_sum(taps(gathered[:1], 2)), SLAB, [(i + 1, i) for i in range(lax.axis_size(SLAB) - 1)])

    def local_subset(x, which):
        shaped = x.reshape(x.shape[0], x.shape[1], per_chan, n_lo, piece)
        taken = lax.dynamic_index_in_dim(shaped, which, axis=3, keepdims=False)
        return taken.reshape(x.shape[0], x.shape[1], per_chan * piece)

    raw6 = jnp.concatenate(
        [shift_rows(image[-1:], upward=False), image, shift_rows(image[:1], upward=True)], axis=0
    )
    send_rows = lax.dynamic_slice_in_dim(raw6, 2 * lo, height, axis=0)
    sent_img = lax.ppermute(local_subset(send_rows, 1 - lo), "lo", [(0, 1), (1, 0)])
    own_img = local_subset(raw6, lo)
    block_piece = lax.dynamic_slice_in_dim(
        jnp.concatenate([sent_img, own_img, sent_img], axis=0), height * (1 - lo), 2 * height + 2, axis=0
    )
    img_block = lax.all_gather(block_piece, "chan", axis=2, tiled=True)

    interior = taps(gathered, 1)
    interior = interior + jnp.pad(taps(gathered[:-1], 0), ((1, 0), (0, 0), (0, 0), (0, 0)))
    interior = interior + jnp.pad(taps(gathered[1:], 2), ((0, 1), (0, 0), (0, 0), (0, 0)))
    conv_sum = shift_sum(interior)
    conv_sum = conv_sum + jnp.concatenate(
        [to_next, jnp.zeros((height - 2, breadth, local_filters), jnp.float32), to_prev], axis=0
    )
    conv_out = conv_sum.astype(jnp.bfloat16)

    conv_wide = conv_out.astype(jnp.float32)
    upstream = grad_filters.astype(jnp.float32)
    partial = jnp.stack(
        [jnp.sum(conv_wide * conv_wide, axis=-1), jnp.sum(upstream * conv_wide, axis=-1)], axis=-1
    )
    totals = lax.psum(partial, "chan")
    inverse_rms = lax.rsqrt(totals[..., 0:1] / all_filters + 1e-06)
    mean_gu = inverse_rms * (totals[..., 1:2] / all_filters)
    unit = conv_wide * inverse_rms
    normed_filters = unit.astype(jnp.bfloat16)
    grad_conv = (inverse_rms * (upstream - unit * mean_gu)).astype(jnp.bfloat16)
    normed = lax.all_to_all(normed_filters, "chan", split_axis=1, concat_axis=2, tiled=True)

    sent_grad = lax.ppermute(grad_conv, "lo", [(0, 1), (1, 0)])
    img_block = jnp.pad(img_block, ((0, 0), (1, 1), (0, 0)))
    width_w = img_block.shape[2]

    def pair_part(grad_rows, first_row):
        flat = grad_rows.reshape(height * breadth, local_filters)
        blocks = []
        for weight_tap_row in range(3):
            rows = lax.dynamic_slice_in_dim(img_block, first_row + weight_tap_row, height, axis=0)
            for weight_tap_col in range(3):
                weight_window = rows[:, weight_tap_col : weight_tap_col + breadth].reshape(height * breadth, width_w)
                blocks.append(
                    lax.dot_general(
                        weight_window,
                        flat,
                        (((0,), (0,)), ((), ())),
                        preferred_element_type=jnp.float32,
                    )
                )
        return jnp.stack(blocks)

    own_part = pair_part(grad_conv, height * lo)
    sent_grad, own_part = lax.optimization_barrier((sent_grad, own_part))
    stacked = (own_part + pair_part(sent_grad, height * (1 - lo))).reshape(3, 3, width_w, local_filters)
    grad_weight = lax.psum_scatter(
        stacked.astype(jnp.bfloat16), "hi", scatter_dimension=2, tiled=True
    ).astype(jnp.float32)

    count = lax.axis_size(SLAB)
    crossing = [(s, s + 1) for s in range(1, count - 1, 2)] + [(s, s - 1) for s in range(2, count, 2)]
    cross = lax.ppermute(jnp.where(lo == 1, grad_conv[-1:], grad_conv[:1]), SLAB, crossing)
    top = jnp.where(lo == 0, cross, sent_grad[-1:])
    bottom = jnp.where(lo == 0, sent_grad[:1], cross)
    grad_rimmed = jnp.concatenate([top, grad_conv, bottom], axis=0)
    grad_padded = jnp.pad(grad_rimmed, ((0, 0), (1, 1), (0, 0)))
    columns = jnp.concatenate(
        [
            grad_padded[2 - a : 2 - a + height, 2 - b : 2 - b + breadth]
            for a in range(3)
            for b in range(3)
        ],
        axis=-1,
    ).reshape(height * breadth, 9 * local_filters)
    weight_late, _ = lax.optimization_barrier((weight, stacked))
    by_filter = jnp.transpose(weight_late, (0, 1, 3, 2)).reshape(9 * local_filters, all_chans)
    input_term = lax.dot_general(
        by_filter, columns, (((0,), (1,)), ((), ())), preferred_element_type=jnp.float32
    )
    group = all_chans // chans
    split = input_term.astype(jnp.bfloat16).reshape(chans, group, height * breadth)
    received = lax.all_to_all(split, "chan", split_axis=0, concat_axis=0, tiled=True)
    summed = jnp.sum(received.astype(jnp.float32), axis=0)
    grad_input = jnp.transpose(summed).astype(jnp.bfloat16).reshape(height, breadth, group)
    return (normed, grad_input, grad_weight)


def solution(mesh):
    slabs = mesh.shape["slab"]
    chans = mesh.shape["chan"]
    split_mesh = Mesh(mesh.devices.reshape(slabs // 2, 2, chans), ("hi", "lo", "chan"))
    return jax.shard_map(
        on_device,
        mesh=split_mesh,
        in_specs=(P(SLAB, None, "chan"), P(None, None, None, "chan"), P(SLAB, "chan", None)),
        out_specs=(P(SLAB, "chan", None), P(SLAB, None, "chan"), P(None, None, SLAB, "chan")),
        check_vma=False,
    )
```

```python
import jax
import jax.numpy as jnp
from jax import lax
from jax.sharding import Mesh
from jax.sharding import PartitionSpec as P

SLAB = ("hi", "lo")


def shift_rows(rows, upward):
    count = lax.axis_size(SLAB)
    if upward:
        pairs = [((i + 1), i) for i in range(count - 1)]
    else:
        pairs = [(i, i + 1) for i in range(count - 1)]
    return lax.ppermute(rows, SLAB, pairs)


def shift_sum(z):
    breadth = z.shape[-3]
    widths = [(0, 0)] * (z.ndim - 3) + [(1, 1), (0, 0), (0, 0)]
    zp = jnp.pad(z, widths)
    return zp[..., 0:breadth, 0, :] + zp[..., 1 : breadth + 1, 1, :] + zp[..., 2 : breadth + 2, 2, :]


def on_device(image, weight, grad_out):
    height = image.shape[0]
    breadth = image.shape[1]
    local_chans = image.shape[2]
    all_chans = weight.shape[2]
    local_filters = weight.shape[3]
    chans = lax.axis_size("chan")
    all_filters = local_filters * chans
    n_hi = lax.axis_size("hi")
    n_lo = lax.axis_size("lo")
    lo = lax.axis_index("lo")
    piece = all_chans // (n_hi * n_lo)
    per_chan = local_chans // (n_lo * piece)

    grad_filters = lax.all_to_all(grad_out, "chan", split_axis=2, concat_axis=1, tiled=True)
    gathered = lax.all_gather(image, "chan", axis=2, tiled=True)

    by_row = jnp.transpose(weight, (0, 2, 1, 3)).reshape(3, all_chans, 3 * local_filters)

    def taps(rows, a):
        count = rows.shape[0]
        flat = rows.reshape(count * breadth, all_chans)
        out = jnp.dot(flat, by_row[a], preferred_element_type=jnp.float32)
        return out.reshape(count, breadth, 3, local_filters)

    to_next = lax.ppermute(shift_sum(taps(gathered[-1:], 0)), SLAB, [(i, i + 1) for i in range(lax.axis_size(SLAB) - 1)])
    to_prev = lax.ppermute(shift_sum(taps(gathered[:1], 2)), SLAB, [(i + 1, i) for i in range(lax.axis_size(SLAB) - 1)])

    def local_subset(x, which):
        shaped = x.reshape(x.shape[0], x.shape[1], per_chan, n_lo, piece)
        taken = lax.dynamic_index_in_dim(shaped, which, axis=3, keepdims=False)
        return taken.reshape(x.shape[0], x.shape[1], per_chan * piece)

    raw6 = jnp.concatenate(
        [shift_rows(image[-1:], upward=False), image, shift_rows(image[:1], upward=True)], axis=0
    )
    send_rows = lax.dynamic_slice_in_dim(raw6, 2 * lo, height, axis=0)
    sent_img = lax.ppermute(local_subset(send_rows, 1 - lo), "lo", [(0, 1), (1, 0)])
    own_img = local_subset(raw6, lo)
    block_piece = lax.dynamic_slice_in_dim(
        jnp.concatenate([sent_img, own_img, sent_img], axis=0), height * (1 - lo), 2 * height + 2, axis=0
    )
    img_block = lax.all_gather(block_piece, "chan", axis=2, tiled=True)

    interior = taps(gathered, 1)
    interior = interior + jnp.pad(taps(gathered[:-1], 0), ((1, 0), (0, 0), (0, 0), (0, 0)))
    interior = interior + jnp.pad(taps(gathered[1:], 2), ((0, 1), (0, 0), (0, 0), (0, 0)))
    conv_sum = shift_sum(interior)
    conv_sum = conv_sum + jnp.concatenate(
        [to_next, jnp.zeros((height - 2, breadth, local_filters), jnp.float32), to_prev], axis=0
    )
    conv_out = conv_sum.astype(jnp.bfloat16)

    conv_wide = conv_out.astype(jnp.float32)
    upstream = grad_filters.astype(jnp.float32)
    partial = jnp.stack(
        [jnp.sum(conv_wide * conv_wide, axis=-1), jnp.sum(upstream * conv_wide, axis=-1)], axis=-1
    )
    totals = lax.psum(partial, "chan")
    inverse_rms = lax.rsqrt(totals[..., 0:1] / all_filters + 1e-06)
    mean_gu = inverse_rms * (totals[..., 1:2] / all_filters)
    unit = conv_wide * inverse_rms
    normed_filters = unit.astype(jnp.bfloat16)
    grad_conv = (inverse_rms * (upstream - unit * mean_gu)).astype(jnp.bfloat16)
    normed = lax.all_to_all(normed_filters, "chan", split_axis=1, concat_axis=2, tiled=True)

    sent_grad = lax.ppermute(grad_conv, "lo", [(0, 1), (1, 0)])
    img_block = jnp.pad(img_block, ((0, 0), (1, 1), (0, 0)))
    width_w = img_block.shape[2]

    def pair_part(grad_rows, first_row):
        flat = grad_rows.reshape(height * breadth, local_filters)
        blocks = []
        for weight_tap_row in range(3):
            rows = lax.dynamic_slice_in_dim(img_block, first_row + weight_tap_row, height, axis=0)
            for weight_tap_col in range(3):
                weight_window = rows[:, weight_tap_col : weight_tap_col + breadth].reshape(height * breadth, width_w)
                blocks.append(
                    lax.dot_general(
                        weight_window,
                        flat,
                        (((0,), (0,)), ((), ())),
                        preferred_element_type=jnp.float32,
                    )
                )
        return jnp.stack(blocks)

    own_part = pair_part(grad_conv, height * lo)
    sent_grad, own_part = lax.optimization_barrier((sent_grad, own_part))
    partner_part = pair_part(sent_grad, height * (1 - lo))
    stacked = jnp.stack(
        [(partner_part[t] + own_part[t]).astype(jnp.bfloat16) for t in range(9)]
    ).reshape(3, 3, width_w, local_filters)
    grad_weight = lax.psum_scatter(stacked, "hi", scatter_dimension=2, tiled=True).astype(jnp.float32)

    count = lax.axis_size(SLAB)
    crossing = [(s, s + 1) for s in range(1, count - 1, 2)] + [(s, s - 1) for s in range(2, count, 2)]
    cross = lax.ppermute(jnp.where(lo == 1, grad_conv[-1:], grad_conv[:1]), SLAB, crossing)
    top = jnp.where(lo == 0, cross, sent_grad[-1:])
    bottom = jnp.where(lo == 0, sent_grad[:1], cross)
    grad_rimmed = jnp.concatenate([top, grad_conv, bottom], axis=0)
    grad_padded = jnp.pad(grad_rimmed, ((0, 0), (1, 1), (0, 0)))
    columns = jnp.concatenate(
        [
            grad_padded[2 - a : 2 - a + height, 2 - b : 2 - b + breadth]
            for a in range(3)
            for b in range(3)
        ],
        axis=-1,
    ).reshape(height * breadth, 9 * local_filters)
    by_filter = jnp.transpose(weight, (0, 1, 3, 2)).reshape(9 * local_filters, all_chans)
    input_term = lax.dot_general(
        by_filter, columns, (((0,), (1,)), ((), ())), preferred_element_type=jnp.float32
    )
    group = all_chans // chans
    split = input_term.astype(jnp.bfloat16).reshape(chans, group, height * breadth)
    received = lax.all_to_all(split, "chan", split_axis=0, concat_axis=0, tiled=True)
    summed = jnp.sum(received.astype(jnp.float32), axis=0)
    grad_input = jnp.transpose(summed).astype(jnp.bfloat16).reshape(height, breadth, group)
    return (normed, grad_input, grad_weight)


def solution(mesh):
    slabs = mesh.shape["slab"]
    chans = mesh.shape["chan"]
    split_mesh = Mesh(mesh.devices.reshape(slabs // 2, 2, chans), ("hi", "lo", "chan"))
    return jax.shard_map(
        on_device,
        mesh=split_mesh,
        in_specs=(P(SLAB, None, "chan"), P(None, None, None, "chan"), P(SLAB, "chan", None)),
        out_specs=(P(SLAB, "chan", None), P(SLAB, None, "chan"), P(None, None, SLAB, "chan")),
        check_vma=False,
    )
```

```python
import jax
import jax.numpy as jnp
from jax import lax
from jax.sharding import Mesh
from jax.sharding import PartitionSpec as P

SLAB = ("hi", "lo")


def shift_rows(rows, upward):
    count = lax.axis_size(SLAB)
    if upward:
        pairs = [((i + 1), i) for i in range(count - 1)]
    else:
        pairs = [(i, i + 1) for i in range(count - 1)]
    return lax.ppermute(rows, SLAB, pairs)


def shift_sum(z):
    breadth = z.shape[-3]
    widths = [(0, 0)] * (z.ndim - 3) + [(1, 1), (0, 0), (0, 0)]
    zp = jnp.pad(z, widths)
    return zp[..., 0:breadth, 0, :] + zp[..., 1 : breadth + 1, 1, :] + zp[..., 2 : breadth + 2, 2, :]


def on_device(image, weight, grad_out):
    height = image.shape[0]
    breadth = image.shape[1]
    local_chans = image.shape[2]
    all_chans = weight.shape[2]
    local_filters = weight.shape[3]
    chans = lax.axis_size("chan")
    all_filters = local_filters * chans
    n_hi = lax.axis_size("hi")
    n_lo = lax.axis_size("lo")
    lo = lax.axis_index("lo")
    piece = all_chans // (n_hi * n_lo)
    per_chan = local_chans // (n_lo * piece)

    grad_filters = lax.all_to_all(grad_out, "chan", split_axis=2, concat_axis=1, tiled=True)
    gathered = lax.all_gather(image, "chan", axis=2, tiled=True)

    by_row = jnp.transpose(weight, (0, 2, 1, 3)).reshape(3, all_chans, 3 * local_filters)

    def taps(rows, a):
        count = rows.shape[0]
        flat = rows.reshape(count * breadth, all_chans)
        out = jnp.dot(flat, by_row[a], preferred_element_type=jnp.float32)
        return out.reshape(count, breadth, 3, local_filters)

    to_next = lax.ppermute(shift_sum(taps(gathered[-1:], 0)), SLAB, [(i, i + 1) for i in range(lax.axis_size(SLAB) - 1)])
    to_prev = lax.ppermute(shift_sum(taps(gathered[:1], 2)), SLAB, [(i + 1, i) for i in range(lax.axis_size(SLAB) - 1)])

    def local_subset(x, which):
        shaped = x.reshape(x.shape[0], x.shape[1], per_chan, n_lo, piece)
        taken = lax.dynamic_index_in_dim(shaped, which, axis=3, keepdims=False)
        return taken.reshape(x.shape[0], x.shape[1], per_chan * piece)

    raw6 = jnp.concatenate(
        [shift_rows(image[-1:], upward=False), image, shift_rows(image[:1], upward=True)], axis=0
    )
    send_rows = lax.dynamic_slice_in_dim(raw6, 2 * lo, height, axis=0)
    sent_img = lax.ppermute(local_subset(send_rows, 1 - lo), "lo", [(0, 1), (1, 0)])
    own_img = local_subset(raw6, lo)
    block_piece = lax.dynamic_slice_in_dim(
        jnp.concatenate([sent_img, own_img, sent_img], axis=0), height * (1 - lo), 2 * height + 2, axis=0
    )
    img_block = lax.all_gather(block_piece, "chan", axis=2, tiled=True)

    interior = taps(gathered, 1)
    interior = interior + jnp.pad(taps(gathered[:-1], 0), ((1, 0), (0, 0), (0, 0), (0, 0)))
    interior = interior + jnp.pad(taps(gathered[1:], 2), ((0, 1), (0, 0), (0, 0), (0, 0)))
    conv_sum = shift_sum(interior)
    conv_sum = conv_sum + jnp.concatenate(
        [to_next, jnp.zeros((height - 2, breadth, local_filters), jnp.float32), to_prev], axis=0
    )
    conv_out = conv_sum.astype(jnp.bfloat16)

    conv_wide = conv_out.astype(jnp.float32)
    upstream = grad_filters.astype(jnp.float32)
    partial = jnp.stack(
        [jnp.sum(conv_wide * conv_wide, axis=-1), jnp.sum(upstream * conv_wide, axis=-1)], axis=-1
    )
    totals = lax.psum(partial, "chan")
    inverse_rms = lax.rsqrt(totals[..., 0:1] / all_filters + 1e-06)
    mean_gu = inverse_rms * (totals[..., 1:2] / all_filters)
    unit = conv_wide * inverse_rms
    normed_filters = unit.astype(jnp.bfloat16)
    grad_conv = (inverse_rms * (upstream - unit * mean_gu)).astype(jnp.bfloat16)
    normed = lax.all_to_all(normed_filters, "chan", split_axis=1, concat_axis=2, tiled=True)

    half = height // 2
    sent_grad = jnp.concatenate(
        [lax.ppermute(grad_conv[:half], "lo", [(0, 1), (1, 0)]), lax.ppermute(grad_conv[half:], "lo", [(0, 1), (1, 0)])],
        axis=0,
    )
    img_block = jnp.pad(img_block, ((0, 0), (1, 1), (0, 0)))
    width_w = img_block.shape[2]

    def pair_part(grad_rows, first_row):
        flat = grad_rows.reshape(height * breadth, local_filters)
        blocks = []
        for weight_tap_row in range(3):
            rows = lax.dynamic_slice_in_dim(img_block, first_row + weight_tap_row, height, axis=0)
            for weight_tap_col in range(3):
                weight_window = rows[:, weight_tap_col : weight_tap_col + breadth].reshape(height * breadth, width_w)
                blocks.append(
                    lax.dot_general(
                        weight_window,
                        flat,
                        (((0,), (0,)), ((), ())),
                        preferred_element_type=jnp.float32,
                    )
                )
        return jnp.stack(blocks)

    own_part = pair_part(grad_conv, height * lo)
    sent_grad, own_part = lax.optimization_barrier((sent_grad, own_part))
    partner_part = pair_part(sent_grad, height * (1 - lo))
    stacked = jnp.stack(
        [(partner_part[t] + own_part[t]).astype(jnp.bfloat16) for t in range(9)]
    ).reshape(3, 3, width_w, local_filters)
    grad_weight = lax.psum_scatter(stacked, "hi", scatter_dimension=2, tiled=True).astype(jnp.float32)

    count = lax.axis_size(SLAB)
    crossing = [(s, s + 1) for s in range(1, count - 1, 2)] + [(s, s - 1) for s in range(2, count, 2)]
    cross = lax.ppermute(jnp.where(lo == 1, grad_conv[-1:], grad_conv[:1]), SLAB, crossing)
    top = jnp.where(lo == 0, cross, sent_grad[-1:])
    bottom = jnp.where(lo == 0, sent_grad[:1], cross)
    grad_rimmed = jnp.concatenate([top, grad_conv, bottom], axis=0)
    grad_padded = jnp.pad(grad_rimmed, ((0, 0), (1, 1), (0, 0)))
    columns = jnp.concatenate(
        [
            grad_padded[2 - a : 2 - a + height, 2 - b : 2 - b + breadth]
            for a in range(3)
            for b in range(3)
        ],
        axis=-1,
    ).reshape(height * breadth, 9 * local_filters)
    by_filter = jnp.transpose(weight, (0, 1, 3, 2)).reshape(9 * local_filters, all_chans)
    input_term = lax.dot_general(
        by_filter, columns, (((0,), (1,)), ((), ())), preferred_element_type=jnp.float32
    )
    group = all_chans // chans
    split = input_term.astype(jnp.bfloat16).reshape(chans, group, height * breadth)
    received = lax.all_to_all(split, "chan", split_axis=0, concat_axis=0, tiled=True)
    summed = jnp.sum(received.astype(jnp.float32), axis=0)
    grad_input = jnp.transpose(summed).astype(jnp.bfloat16).reshape(height, breadth, group)
    return (normed, grad_input, grad_weight)


def solution(mesh):
    slabs = mesh.shape["slab"]
    chans = mesh.shape["chan"]
    split_mesh = Mesh(mesh.devices.reshape(slabs // 2, 2, chans), ("hi", "lo", "chan"))
    return jax.shard_map(
        on_device,
        mesh=split_mesh,
        in_specs=(P(SLAB, None, "chan"), P(None, None, None, "chan"), P(SLAB, "chan", None)),
        out_specs=(P(SLAB, "chan", None), P(SLAB, None, "chan"), P(None, None, SLAB, "chan")),
        check_vma=False,
    )
```

```python
import jax
import jax.numpy as jnp
from jax import lax
from jax.sharding import Mesh
from jax.sharding import PartitionSpec as P

SLAB = ("hi", "lo")


def shift_rows(rows, upward):
    count = lax.axis_size(SLAB)
    if upward:
        pairs = [((i + 1), i) for i in range(count - 1)]
    else:
        pairs = [(i, i + 1) for i in range(count - 1)]
    return lax.ppermute(rows, SLAB, pairs)


def shift_sum(z):
    breadth = z.shape[-3]
    widths = [(0, 0)] * (z.ndim - 3) + [(1, 1), (0, 0), (0, 0)]
    zp = jnp.pad(z, widths)
    return zp[..., 0:breadth, 0, :] + zp[..., 1 : breadth + 1, 1, :] + zp[..., 2 : breadth + 2, 2, :]


def on_device(image, weight, grad_out):
    height = image.shape[0]
    breadth = image.shape[1]
    local_chans = image.shape[2]
    all_chans = weight.shape[2]
    local_filters = weight.shape[3]
    chans = lax.axis_size("chan")
    all_filters = local_filters * chans
    n_hi = lax.axis_size("hi")
    n_lo = lax.axis_size("lo")
    lo = lax.axis_index("lo")
    piece = all_chans // (n_hi * n_lo)
    per_chan = local_chans // (n_lo * piece)

    grad_filters = lax.all_to_all(grad_out, "chan", split_axis=2, concat_axis=1, tiled=True)
    gathered = lax.all_gather(image, "chan", axis=2, tiled=True)

    by_row = jnp.transpose(weight, (0, 2, 1, 3)).reshape(3, all_chans, 3 * local_filters)

    def taps(rows, a):
        count = rows.shape[0]
        flat = rows.reshape(count * breadth, all_chans)
        out = jnp.dot(flat, by_row[a], preferred_element_type=jnp.float32)
        return out.reshape(count, breadth, 3, local_filters)

    to_next = lax.ppermute(shift_sum(taps(gathered[-1:], 0)), SLAB, [(i, i + 1) for i in range(lax.axis_size(SLAB) - 1)])
    to_prev = lax.ppermute(shift_sum(taps(gathered[:1], 2)), SLAB, [(i + 1, i) for i in range(lax.axis_size(SLAB) - 1)])

    def local_subset(x, which):
        shaped = x.reshape(x.shape[0], x.shape[1], per_chan, n_lo, piece)
        taken = lax.dynamic_index_in_dim(shaped, which, axis=3, keepdims=False)
        return taken.reshape(x.shape[0], x.shape[1], per_chan * piece)

    raw6 = jnp.concatenate(
        [shift_rows(image[-1:], upward=False), image, shift_rows(image[:1], upward=True)], axis=0
    )
    send_rows = lax.dynamic_slice_in_dim(raw6, 2 * lo, height, axis=0)
    sent_img = lax.ppermute(local_subset(send_rows, 1 - lo), "lo", [(0, 1), (1, 0)])
    own_img = local_subset(raw6, lo)
    block_piece = lax.dynamic_slice_in_dim(
        jnp.concatenate([sent_img, own_img, sent_img], axis=0), height * (1 - lo), 2 * height + 2, axis=0
    )
    img_block = lax.all_gather(block_piece, "chan", axis=2, tiled=True)

    interior = taps(gathered, 1)
    interior = interior + jnp.pad(taps(gathered[:-1], 0), ((1, 0), (0, 0), (0, 0), (0, 0)))
    interior = interior + jnp.pad(taps(gathered[1:], 2), ((0, 1), (0, 0), (0, 0), (0, 0)))
    conv_sum = shift_sum(interior)
    conv_sum = conv_sum + jnp.concatenate(
        [to_next, jnp.zeros((height - 2, breadth, local_filters), jnp.float32), to_prev], axis=0
    )
    conv_out = conv_sum.astype(jnp.bfloat16)

    conv_wide = conv_out.astype(jnp.float32)
    upstream = grad_filters.astype(jnp.float32)
    partial = jnp.stack(
        [jnp.sum(conv_wide * conv_wide, axis=-1), jnp.sum(upstream * conv_wide, axis=-1)], axis=-1
    )
    totals = lax.psum(partial, "chan")
    inverse_rms = lax.rsqrt(totals[..., 0:1] / all_filters + 1e-06)
    mean_gu = inverse_rms * (totals[..., 1:2] / all_filters)
    unit = conv_wide * inverse_rms
    normed_filters = unit.astype(jnp.bfloat16)
    grad_conv = (inverse_rms * (upstream - unit * mean_gu)).astype(jnp.bfloat16)
    normed = lax.all_to_all(normed_filters, "chan", split_axis=1, concat_axis=2, tiled=True)

    sent_grad = lax.ppermute(grad_conv, "lo", [(0, 1), (1, 0)])
    img_block = jnp.pad(img_block, ((0, 0), (1, 1), (0, 0)))
    width_w = img_block.shape[2]

    def pair_part(grad_rows, first_row):
        flat = grad_rows.reshape(height * breadth, local_filters)
        blocks = []
        for weight_tap_row in range(3):
            rows = lax.dynamic_slice_in_dim(img_block, first_row + weight_tap_row, height, axis=0)
            for weight_tap_col in range(3):
                weight_window = rows[:, weight_tap_col : weight_tap_col + breadth].reshape(height * breadth, width_w)
                blocks.append(
                    lax.dot_general(
                        weight_window,
                        flat,
                        (((0,), (0,)), ((), ())),
                        preferred_element_type=jnp.float32,
                    )
                )
        return jnp.stack(blocks)

    own_part = pair_part(grad_conv, height * lo)
    sent_grad, own_part = lax.optimization_barrier((sent_grad, own_part))
    stacked = jnp.transpose(own_part + pair_part(sent_grad, height * (1 - lo)), (1, 0, 2))
    scattered = lax.psum_scatter(stacked.astype(jnp.bfloat16), "hi", scatter_dimension=0, tiled=True)
    grad_weight = jnp.transpose(scattered, (1, 0, 2)).astype(jnp.float32).reshape(
        3, 3, scattered.shape[0], local_filters
    )

    count = lax.axis_size(SLAB)
    crossing = [(s, s + 1) for s in range(1, count - 1, 2)] + [(s, s - 1) for s in range(2, count, 2)]
    cross = lax.ppermute(jnp.where(lo == 1, grad_conv[-1:], grad_conv[:1]), SLAB, crossing)
    top = jnp.where(lo == 0, cross, sent_grad[-1:])
    bottom = jnp.where(lo == 0, sent_grad[:1], cross)
    grad_rimmed = jnp.concatenate([top, grad_conv, bottom], axis=0)
    grad_padded = jnp.pad(grad_rimmed, ((0, 0), (1, 1), (0, 0)))
    columns = jnp.concatenate(
        [
            grad_padded[2 - a : 2 - a + height, 2 - b : 2 - b + breadth]
            for a in range(3)
            for b in range(3)
        ],
        axis=-1,
    ).reshape(height * breadth, 9 * local_filters)
    by_filter = jnp.transpose(weight, (0, 1, 3, 2)).reshape(9 * local_filters, all_chans)
    input_term = lax.dot_general(
        by_filter, columns, (((0,), (1,)), ((), ())), preferred_element_type=jnp.float32
    )
    group = all_chans // chans
    split = input_term.astype(jnp.bfloat16).reshape(chans, group, height * breadth)
    received = lax.all_to_all(split, "chan", split_axis=0, concat_axis=0, tiled=True)
    summed = jnp.sum(received.astype(jnp.float32), axis=0)
    grad_input = jnp.transpose(summed).astype(jnp.bfloat16).reshape(height, breadth, group)
    return (normed, grad_input, grad_weight)


def solution(mesh):
    slabs = mesh.shape["slab"]
    chans = mesh.shape["chan"]
    split_mesh = Mesh(mesh.devices.reshape(slabs // 2, 2, chans), ("hi", "lo", "chan"))
    return jax.shard_map(
        on_device,
        mesh=split_mesh,
        in_specs=(P(SLAB, None, "chan"), P(None, None, None, "chan"), P(SLAB, "chan", None)),
        out_specs=(P(SLAB, "chan", None), P(SLAB, None, "chan"), P(None, None, SLAB, "chan")),
        check_vma=False,
    )
```

```python
import jax
import jax.numpy as jnp
from jax import lax
from jax.sharding import Mesh
from jax.sharding import PartitionSpec as P

SLAB = ("hi", "lo")


def shift_rows(rows, upward):
    count = lax.axis_size(SLAB)
    if upward:
        pairs = [((i + 1), i) for i in range(count - 1)]
    else:
        pairs = [(i, i + 1) for i in range(count - 1)]
    return lax.ppermute(rows, SLAB, pairs)


def shift_sum(z):
    breadth = z.shape[-3]
    widths = [(0, 0)] * (z.ndim - 3) + [(1, 1), (0, 0), (0, 0)]
    zp = jnp.pad(z, widths)
    return zp[..., 0:breadth, 0, :] + zp[..., 1 : breadth + 1, 1, :] + zp[..., 2 : breadth + 2, 2, :]


def on_device(image, weight, grad_out):
    height = image.shape[0]
    breadth = image.shape[1]
    local_chans = image.shape[2]
    all_chans = weight.shape[2]
    local_filters = weight.shape[3]
    chans = lax.axis_size("chan")
    all_filters = local_filters * chans
    n_hi = lax.axis_size("hi")
    n_lo = lax.axis_size("lo")
    lo = lax.axis_index("lo")
    piece = all_chans // (n_hi * n_lo)
    per_chan = local_chans // (n_lo * piece)

    gathered = lax.all_gather(image, "chan", axis=2, tiled=True)
    grad_late, _ = lax.optimization_barrier((grad_out, gathered))
    grad_filters = lax.all_to_all(grad_late, "chan", split_axis=2, concat_axis=1, tiled=True)

    by_row = jnp.transpose(weight, (0, 2, 1, 3)).reshape(3, all_chans, 3 * local_filters)

    def taps(rows, a):
        count = rows.shape[0]
        flat = rows.reshape(count * breadth, all_chans)
        out = jnp.dot(flat, by_row[a], preferred_element_type=jnp.float32)
        return out.reshape(count, breadth, 3, local_filters)

    to_next = lax.ppermute(shift_sum(taps(gathered[-1:], 0)), SLAB, [(i, i + 1) for i in range(lax.axis_size(SLAB) - 1)])
    to_prev = lax.ppermute(shift_sum(taps(gathered[:1], 2)), SLAB, [(i + 1, i) for i in range(lax.axis_size(SLAB) - 1)])

    def local_subset(x, which):
        shaped = x.reshape(x.shape[0], x.shape[1], per_chan, n_lo, piece)
        taken = lax.dynamic_index_in_dim(shaped, which, axis=3, keepdims=False)
        return taken.reshape(x.shape[0], x.shape[1], per_chan * piece)

    raw6 = jnp.concatenate(
        [shift_rows(image[-1:], upward=False), image, shift_rows(image[:1], upward=True)], axis=0
    )
    send_rows = lax.dynamic_slice_in_dim(raw6, 2 * lo, height, axis=0)
    sent_img = lax.ppermute(local_subset(send_rows, 1 - lo), "lo", [(0, 1), (1, 0)])
    own_img = local_subset(raw6, lo)
    block_piece = lax.dynamic_slice_in_dim(
        jnp.concatenate([sent_img, own_img, sent_img], axis=0), height * (1 - lo), 2 * height + 2, axis=0
    )
    img_block = lax.all_gather(block_piece, "chan", axis=2, tiled=True)

    interior = taps(gathered, 1)
    interior = interior + jnp.pad(taps(gathered[:-1], 0), ((1, 0), (0, 0), (0, 0), (0, 0)))
    interior = interior + jnp.pad(taps(gathered[1:], 2), ((0, 1), (0, 0), (0, 0), (0, 0)))
    conv_sum = shift_sum(interior)
    conv_sum = conv_sum + jnp.concatenate(
        [to_next, jnp.zeros((height - 2, breadth, local_filters), jnp.float32), to_prev], axis=0
    )
    conv_out = conv_sum.astype(jnp.bfloat16)

    conv_wide = conv_out.astype(jnp.float32)
    upstream = grad_filters.astype(jnp.float32)
    partial = jnp.stack(
        [jnp.sum(conv_wide * conv_wide, axis=-1), jnp.sum(upstream * conv_wide, axis=-1)], axis=-1
    )
    totals = lax.psum(partial, "chan")
    inverse_rms = lax.rsqrt(totals[..., 0:1] / all_filters + 1e-06)
    mean_gu = inverse_rms * (totals[..., 1:2] / all_filters)
    unit = conv_wide * inverse_rms
    normed_filters = unit.astype(jnp.bfloat16)
    grad_conv = (inverse_rms * (upstream - unit * mean_gu)).astype(jnp.bfloat16)
    normed = lax.all_to_all(normed_filters, "chan", split_axis=1, concat_axis=2, tiled=True)

    sent_grad = lax.ppermute(grad_conv, "lo", [(0, 1), (1, 0)])
    img_block = jnp.pad(img_block, ((0, 0), (1, 1), (0, 0)))
    width_w = img_block.shape[2]

    def pair_part(grad_rows, first_row):
        flat = grad_rows.reshape(height * breadth, local_filters)
        blocks = []
        for weight_tap_row in range(3):
            rows = lax.dynamic_slice_in_dim(img_block, first_row + weight_tap_row, height, axis=0)
            for weight_tap_col in range(3):
                weight_window = rows[:, weight_tap_col : weight_tap_col + breadth].reshape(height * breadth, width_w)
                blocks.append(
                    lax.dot_general(
                        weight_window,
                        flat,
                        (((0,), (0,)), ((), ())),
                        preferred_element_type=jnp.float32,
                    )
                )
        return jnp.stack(blocks)

    own_part = pair_part(grad_conv, height * lo)
    sent_grad, own_part = lax.optimization_barrier((sent_grad, own_part))
    stacked = (own_part + pair_part(sent_grad, height * (1 - lo))).reshape(3, 3, width_w, local_filters)
    grad_weight = lax.psum_scatter(
        stacked.astype(jnp.bfloat16), "hi", scatter_dimension=2, tiled=True
    ).astype(jnp.float32)

    count = lax.axis_size(SLAB)
    crossing = [(s, s + 1) for s in range(1, count - 1, 2)] + [(s, s - 1) for s in range(2, count, 2)]
    cross = lax.ppermute(jnp.where(lo == 1, grad_conv[-1:], grad_conv[:1]), SLAB, crossing)
    top = jnp.where(lo == 0, cross, sent_grad[-1:])
    bottom = jnp.where(lo == 0, sent_grad[:1], cross)
    grad_rimmed = jnp.concatenate([top, grad_conv, bottom], axis=0)
    grad_padded = jnp.pad(grad_rimmed, ((0, 0), (1, 1), (0, 0)))
    columns = jnp.concatenate(
        [
            grad_padded[2 - a : 2 - a + height, 2 - b : 2 - b + breadth]
            for a in range(3)
            for b in range(3)
        ],
        axis=-1,
    ).reshape(height * breadth, 9 * local_filters)
    by_filter = jnp.transpose(weight, (0, 1, 3, 2)).reshape(9 * local_filters, all_chans)
    input_term = lax.dot_general(
        by_filter, columns, (((0,), (1,)), ((), ())), preferred_element_type=jnp.float32
    )
    group = all_chans // chans
    split = input_term.astype(jnp.bfloat16).reshape(chans, group, height * breadth)
    received = lax.all_to_all(split, "chan", split_axis=0, concat_axis=0, tiled=True)
    summed = jnp.sum(received.astype(jnp.float32), axis=0)
    grad_input = jnp.transpose(summed).astype(jnp.bfloat16).reshape(height, breadth, group)
    return (normed, grad_input, grad_weight)


def solution(mesh):
    slabs = mesh.shape["slab"]
    chans = mesh.shape["chan"]
    split_mesh = Mesh(mesh.devices.reshape(slabs // 2, 2, chans), ("hi", "lo", "chan"))
    return jax.shard_map(
        on_device,
        mesh=split_mesh,
        in_specs=(P(SLAB, None, "chan"), P(None, None, None, "chan"), P(SLAB, "chan", None)),
        out_specs=(P(SLAB, "chan", None), P(SLAB, None, "chan"), P(None, None, SLAB, "chan")),
        check_vma=False,
    )
```
